256 devices in a mesh: ka: 64 (over z, y, core), pb: 4 (over x).
Axes of the slice: x: 4, y: 4, z: 8, core: 2. Of those that a mesh axis runs over, the one named last changes fastest.
Arguments:
- occupation: float32 [6, 262144], P(None, 'ka'), may hold values from 0 to 1
- gain_table: bfloat16 [64, 36, 262144], P('pb', None, 'ka'), may hold values from 0.0049743652 to 0.19921875
- loss_table: bfloat16 [64, 36, 262144], P('pb', None, 'ka'), may hold values from 0.0049743652 to 0.19921875
- owner: int32 [4, 64, 16, 32, 1], P('pb', 'ka'), may hold values from 0 to 63; in each aligned block of 512 rows (0 to 511, 512 to 1023, ..., all dimensions but the last counted through in order) at most 16 rows name the same one
- local_index: int32 [4, 64, 16, 32], P('pb', 'ka'), may hold values from 0 to 31
- pair_mask: int32 [64, 36], P('pb'), may hold values 0 or 1
- counts: int32 [4, 64], P('pb', 'ka'), may hold values from 1 to 16, as said below
Outputs:
- collision: float32 [6, 262144], P(None, ('ka', 'pb'))
- section_occupation: float32 [6, 262144], P(None, ('ka', 'pb'))
The draws below stay inside these ranges and needn't reach their ends.
Inputs may be any that keep to these rules, and one draw needn't show every extreme that they name: Among the 16 x 32 entries of one q-shift group and one k-block, no owner is named more than 16 times. The active q-shifts of a group at a k-block are its first counts ones.
All inputs are finite; a program needn't handle non-finite values. No bound on the sum of `pair_mask` on one device may be relied on, other than what follows from the above.
Results may differ from the reference program's by a relative error of at most 0.0003.
Values sent between devices are 32-bit elements; how exact they have to be, the bound alone decides.
No kernel may reach another device: no remote copies, remote signals or barrier semaphores. Data moves between devices by JAX's collectives and lax.ppermute only.
A program may use at most 128 MiB of HBM per device.

```python
import math
import jax
import jax.numpy as jnp
import numpy as np
from jax import lax

BANDS = 6
PAIRS = 36
KDEV = 4096
KSUB = 128
S_DEV = 16
NSUB = 32
SHIFTS = 64
KPTS = 262144
CAP = 16
N_KA = 64
N_PB = 4


def draw_counts(key, part):
    values = jax.random.randint(key, (N_PB * N_KA,), 1, S_DEV + 1)
    position = jax.random.randint(jax.random.fold_in(key, 7), (), 0, N_PB * N_KA)
    values = values.at[position].set(S_DEV)
    return values.reshape(N_PB, N_KA).astype(jnp.int32)


def place_ends(values, stream_key, smallest, largest):
    dims = values.shape
    index_at = [jax.random.randint(jax.random.fold_in(stream_key, axis), (), 0, dims[axis]) for axis in range(len(dims))]
    values = values.at[tuple(index_at)].set(smallest)
    longest = dims.index(max(dims))
    index_at[longest] = (index_at[longest] + 1) % dims[longest]
    return values.at[tuple(index_at)].set(largest)


def level_of(rng, extent, split, low, top_value):
    def one(dim, blocks):
        steps = jax.random.uniform(jax.random.fold_in(jax.random.fold_in(rng, 6), dim), (blocks,), jnp.float32, low / len(split), top_value / len(split))
        return jnp.repeat(jnp.exp(steps), extent[dim] // blocks).reshape((-1,) + (1,) * (len(extent) - dim - 1))

    gain = one(*split[0])
    for cut in split[1:]:
        gain = gain * one(*cut)
    return gain


def deal_out(rng, own, number, rows, count, top, most, skew):
    sequence = jax.random.permutation(rng, count)
    heavy_load, common = portions_of(count, rows * top, most, skew, True), portions_of(count, rows * top, most, skew, False)
    places = jnp.arange(count)

    def named(sizes, turn):
        used = int((sizes > 0).sum())
        fixed = max(1, used // 4)
        moved = fixed + (places - fixed + turn * (used - fixed)) % max(1, count - fixed)
        return jnp.zeros((count,), jnp.int32).at[sequence[jnp.where(places < fixed, places, moved)]].set(jnp.asarray(sizes, jnp.int32))

    sizes = jnp.where(number % 4 == 0, named(heavy_load, number // 4), named(common, number - number // 4 - 1))
    mixed = jax.random.permutation(jax.random.fold_in(own, 3), count)
    source_of, sink = mixed[0:count // 2 * 2:2], mixed[1:count // 2 * 2:2]
    margin = jnp.minimum(sizes[source_of] - 1, most - sizes[sink]) // 2
    margin = jnp.where((source_of == sequence[0]) | (sink == sequence[0]) | (sizes[sink] == 0), 0, jnp.maximum(margin, 0))
    moved = jax.random.randint(jax.random.fold_in(own, 4), (count // 2,), 0, 1 << 20) % (margin + 1)
    sizes = sizes.at[source_of].add(-moved).at[sink].add(moved)
    labels = jnp.searchsorted(jnp.cumsum(sizes), jnp.arange(rows * top), side="right").astype(jnp.int32)
    table = labels.reshape(top, rows).T
    table = table[jax.random.permutation(jax.random.fold_in(own, 1), rows)]
    turn = jax.random.randint(jax.random.fold_in(own, 2), (rows, 1), 0, top)
    return jnp.take_along_axis(table, (jnp.arange(top)[None, :] + turn) % top, axis=1)


def portions_of(amount, total, reach, lean, full):
    weights = [(1 << 20) // math.isqrt(grade ** lean) + 1 for grade in range(1, amount + 1)]
    largest = reach if full else min(reach, max(-(-total // amount), total * weights[0] // sum(weights)))
    least = 1 if total - largest >= amount - 1 else 0
    holding, surplus = [largest] + [least] * (amount - 1), total - largest - least * (amount - 1)
    while surplus > 0:
        movable = [i for i in range(1, amount) if holding[i] < largest] or [i for i in range(1, amount) if holding[i] < reach]
        mass, left = sum([weights[i] for i in movable]), surplus
        for i in movable:
            extra = min(reach - holding[i], max(1, left * weights[i] // mass), surplus)
            holding[i] = holding[i] + extra
            surplus = surplus - extra
    return np.array(holding)


def setup_inputs(seed: int = 0) -> dict:
    key_list = jax.random.split(jax.random.key(seed), 8)
    occupation = jnp.clip(1.0 * jax.random.uniform(key_list[0], (BANDS, KPTS), jnp.float32) ** level_of(key_list[0], (BANDS, KPTS), ((1, 64),), -0.2, 0.2), 0.0, 1.0)
    gain_table = jnp.clip(jnp.exp(math.log(0.19921875) - 3.6901057 * jax.random.uniform(key_list[1], (SHIFTS, PAIRS, KPTS), jnp.float32) ** level_of(key_list[1], (SHIFTS, PAIRS, KPTS), ((0, 4), (2, 64)), -0.2, 0.2)), 0.0049743652, 0.19921875).astype(jnp.bfloat16)
    loss_table = jnp.clip(jnp.exp(math.log(0.19921875) - 3.6901057 * jax.random.uniform(key_list[2], (SHIFTS, PAIRS, KPTS), jnp.float32) ** level_of(key_list[2], (SHIFTS, PAIRS, KPTS), ((0, 4), (2, 64)), -0.2, 0.2)), 0.0049743652, 0.19921875).astype(jnp.bfloat16)
    owner_keys = jax.random.split(jax.random.fold_in(key_list[3], 1), N_PB * N_KA * S_DEV * NSUB // (S_DEV * NSUB))
    owner_turns = jax.random.permutation(jax.random.fold_in(key_list[3], 3), N_PB * N_KA * S_DEV * NSUB // (S_DEV * NSUB))
    owner = jax.vmap(lambda own, number: deal_out(jax.random.fold_in(key_list[3], 2), own, number, S_DEV * NSUB, N_KA, 1, CAP, 2))(owner_keys, owner_turns).reshape((N_PB, N_KA, S_DEV, NSUB, 1))
    local_index = place_ends(jax.random.randint(key_list[4], (N_PB, N_KA, S_DEV, NSUB), 0, NSUB), jax.random.fold_in(key_list[4], 1), 0, NSUB - 1).astype(jnp.int32)
    pair_mask = place_ends((jax.random.randint(key_list[5], (SHIFTS, PAIRS), 0, 2) < 1).astype(jnp.int32), jax.random.fold_in(key_list[5], 1), 0, 1)
    counts = draw_counts(jax.random.fold_in(key_list[7], 71), 0)
    return {"occupation": occupation, "gain_table": gain_table, "loss_table": loss_table, "owner": owner, "local_index": local_index, "pair_mask": pair_mask, "counts": counts}


half_step = 0.5


def reference(occupation, gain_table, loss_table, owner, local_index, pair_mask, counts):
    sub_count = KDEV // KSUB
    sources = owner[..., 0] * sub_count + local_index
    sources = sources.transpose(0, 2, 1, 3).reshape(SHIFTS, N_KA * sub_count).astype(jnp.int32)
    active = (jnp.arange(S_DEV, dtype=jnp.int32)[None, :, None] < counts[:, None, :]).astype(jnp.float32)
    active = active.reshape(SHIFTS, N_KA)
    blocks = occupation.reshape(BANDS, N_KA * sub_count, KSUB)

    def one_shift(carry, inputs):
        gains, losses, source_row, mask_row, active_row = inputs
        shifted = blocks[:, source_row, :].reshape(BANDS, KPTS)
        weight = mask_row.astype(jnp.float32)[:, None] * jnp.repeat(active_row, KDEV)[None, :]
        gain_four = (gains.astype(jnp.float32) * weight).reshape(BANDS, BANDS, KPTS)
        loss_four = (losses.astype(jnp.float32) * weight).reshape(BANDS, BANDS, KPTS)
        inflow = jnp.sum(gain_four * shifted[None, :, :], axis=1)
        outflow = jnp.sum(loss_four * (1.0 - shifted)[None, :, :], axis=1)
        inflow_total, outflow_total = carry
        return (inflow_total + inflow, outflow_total + outflow), None

    start = (jnp.zeros((BANDS, KPTS), jnp.float32), jnp.zeros((BANDS, KPTS), jnp.float32))
    (inflow, outflow), unused = lax.scan(one_shift, start, (gain_table, loss_table, sources, pair_mask, active))
    collision = (1.0 - occupation) * inflow - occupation * outflow
    return collision, occupation + half_step * collision
```

```python
import jax
import jax.numpy as jnp
from jax import lax
from jax.sharding import PartitionSpec as P

half_step = 0.5


def body(occupation, gain_table, loss_table, owner, local_index, pair_mask, counts):
    bands, width = occupation.shape
    shifts = gain_table.shape[0]
    sub_count = local_index.shape[3]
    sub_width = width // sub_count
    ka_count = lax.axis_size("ka")
    pb_count = lax.axis_size("pb")
    total_requests = shifts * sub_count
    cap = shifts
    owners = owner.reshape(total_requests)
    sources = local_index.reshape(total_requests)

    hits = (owners[:, None] == jnp.arange(ka_count, dtype=jnp.int32)[None, :]).astype(jnp.float32)
    earlier = (
        jnp.arange(total_requests, dtype=jnp.int32)[:, None]
        > jnp.arange(total_requests, dtype=jnp.int32)[None, :]
    ).astype(jnp.float32)
    before = jnp.dot(earlier, hits, preferred_element_type=jnp.float32)
    slot = jnp.sum(before * hits, axis=1).astype(jnp.int32)
    place = owners * cap + slot

    wanted = jnp.zeros((ka_count * cap,), jnp.int32).at[place].set(sources, unique_indices=True)
    asked = lax.all_to_all(wanted.reshape(ka_count, cap), "ka", 0, 0, tiled=True)

    blocks = occupation.reshape(bands, sub_count, sub_width).transpose(1, 0, 2)
    outgoing = jnp.take(blocks, asked.reshape(ka_count * cap), axis=0)
    incoming = lax.all_to_all(
        outgoing.reshape(ka_count, cap * bands * sub_width), "ka", 0, 0, tiled=True
    ).reshape(ka_count * cap, bands, sub_width)
    picked = jnp.take(incoming, place, axis=0)
    shifted = (
        picked.reshape(shifts, sub_count, bands, sub_width)
        .transpose(0, 2, 1, 3)
        .reshape(shifts, bands, width)
    )
    active = (jnp.arange(shifts, dtype=jnp.int32) < counts.reshape(())).astype(jnp.float32)
    weight = pair_mask.astype(jnp.float32) * active[:, None]
    gain_four = (gain_table.astype(jnp.float32) * weight[:, :, None]).reshape(
        shifts, bands, bands, width
    )
    loss_four = (loss_table.astype(jnp.float32) * weight[:, :, None]).reshape(
        shifts, bands, bands, width
    )
    inflow = jnp.einsum("smnk,snk->mk", gain_four, shifted)
    outflow = jnp.einsum("smnk,snk->mk", loss_four, 1.0 - shifted)
    partial_terms = (1.0 - occupation) * inflow - occupation * outflow
    share_width = width // pb_count
    parts = partial_terms.reshape(bands, pb_count, share_width).transpose(1, 0, 2)
    gathered = lax.all_to_all(parts, "pb", 0, 0, tiled=True)
    collision = jnp.sum(gathered, axis=0)
    own_share = lax.dynamic_slice_in_dim(
        occupation, lax.axis_index("pb") * share_width, share_width, 1
    )
    return (collision, own_share + half_step * collision)


def solution(mesh):
    return jax.shard_map(
        body,
        mesh=mesh,
        in_specs=(
            P(None, "ka"),
            P("pb", None, "ka"),
            P("pb", None, "ka"),
            P("pb", "ka", None, None, None),
            P("pb", "ka", None, None),
            P("pb", None),
            P("pb", "ka"),
        ),
        out_specs=(P(None, ("ka", "pb")), P(None, ("ka", "pb"))),
        check_vma=False,
    )
```

```python
import jax
import jax.numpy as jnp
from jax import lax
from jax.sharding import PartitionSpec as P

half_step = 0.5


def ring_gather(block, y_count, z_count):
    ka_count = 2 * y_count * z_count
    per_z = 2 * y_count

    def pairs(fn):
        return [(j, fn(j)) for j in range(ka_count)]

    def y_step(d):
        return pairs(lambda j: (j // per_z) * per_z + ((j // 2 + d) % y_count) * 2 + j % 2)

    def z_step(d):
        return pairs(lambda j: ((j // per_z + d) % z_count) * per_z + j % per_z)

    def ring(x, step, count):
        ahead = {0: x}
        fwd, back = x, x
        for d in range(1, count // 2 + 1):
            back = lax.ppermute(back, "ka", step(-1))
            ahead[d] = back
            if d < count - d:
                fwd = lax.ppermute(fwd, "ka", step(1))
                ahead[count - d] = fwd
        return jnp.stack([ahead[d] for d in range(count)])

    along_y = ring(block, y_step, y_count)
    along_z = ring(along_y, z_step, z_count)
    other = lax.ppermute(along_z, "ka", pairs(lambda j: j ^ 1))
    return jnp.stack([along_z, other])


def body(occupation, gain_table, loss_table, owner, local_index, pair_mask, counts):
    bands, width = occupation.shape
    shifts = gain_table.shape[0]
    sub_count = local_index.shape[3]
    sub_width = width // sub_count
    ka_count = lax.axis_size("ka")
    pb_count = lax.axis_size("pb")
    z_count = 8
    y_count = ka_count // (2 * z_count)
    total_requests = shifts * sub_count

    gathered = ring_gather(occupation, y_count, z_count).reshape(
        ka_count, bands, sub_count, sub_width
    )
    me = lax.axis_index("ka")
    my_z, my_y, my_c = me // (2 * y_count), (me // 2) % y_count, me % 2
    owners = owner.reshape(total_requests)
    o_z, o_y, o_c = owners // (2 * y_count), (owners // 2) % y_count, owners % 2
    where = (
        (o_c ^ my_c) * (z_count * y_count)
        + ((o_z - my_z) % z_count) * y_count
        + (o_y - my_y) % y_count
    )
    sources = local_index.reshape(total_requests)
    picked = gathered[where, :, sources, :]
    shifted = (
        picked.reshape(shifts, sub_count, bands, sub_width)
        .transpose(0, 2, 1, 3)
        .reshape(shifts, bands, width)
    )
    active = (jnp.arange(shifts, dtype=jnp.int32) < counts.reshape(())).astype(jnp.float32)
    weight = pair_mask.astype(jnp.float32) * active[:, None]
    gain_four = (gain_table.astype(jnp.float32) * weight[:, :, None]).reshape(
        shifts, bands, bands, width
    )
    loss_four = (loss_table.astype(jnp.float32) * weight[:, :, None]).reshape(
        shifts, bands, bands, width
    )
    inflow = jnp.einsum("smnk,snk->mk", gain_four, shifted)
    outflow = jnp.einsum("smnk,snk->mk", loss_four, 1.0 - shifted)
    partial_terms = (1.0 - occupation) * inflow - occupation * outflow
    share_width = width // pb_count
    parts = partial_terms.reshape(bands, pb_count, share_width).transpose(1, 0, 2)
    collision = jnp.sum(lax.all_to_all(parts, "pb", 0, 0, tiled=True), axis=0)
    own_share = lax.dynamic_slice_in_dim(
        occupation, lax.axis_index("pb") * share_width, share_width, 1
    )
    return (collision, own_share + half_step * collision)


def solution(mesh):
    return jax.shard_map(
        body,
        mesh=mesh,
        in_specs=(
            P(None, "ka"),
            P("pb", None, "ka"),
            P("pb", None, "ka"),
            P("pb", "ka", None, None, None),
            P("pb", "ka", None, None),
            P("pb", None),
            P("pb", "ka"),
        ),
        out_specs=(P(None, ("ka", "pb")), P(None, ("ka", "pb"))),
        check_vma=False,
    )
```

```python
import functools

import jax
import jax.numpy as jnp
import numpy as np
from jax import lax
from jax.experimental import pallas as pl
from jax.experimental.pallas import tpu as pltpu
from jax.sharding import PartitionSpec as P

half_step = 0.5
HI = lax.Precision.HIGHEST


def collide_kernel(idx_ref, g_ref, e_ref, f_ref, gain_ref, loss_ref, occ_ref, out_ref, *, shifts, nsub, sub_count, lanes):
    t = pl.program_id(0)
    pairs = gain_ref.shape[1]

    def step(s, carry):
        acc_i, acc_o = carry
        base = s * sub_count + t * nsub
        sh = jnp.concatenate([g_ref[idx_ref[base + jj]] for jj in range(nsub)], axis=1)
        both = jnp.concatenate([sh, 1.0 - sh], axis=1)
        spread = jnp.dot(e_ref[s], both, precision=HI, preferred_element_type=jnp.float32)
        acc_i = acc_i + gain_ref[s].astype(jnp.float32) * spread[:, :lanes]
        acc_o = acc_o + loss_ref[s].astype(jnp.float32) * spread[:, lanes:]
        return acc_i, acc_o

    zero = jnp.zeros((pairs, lanes), jnp.float32)
    acc_i, acc_o = lax.fori_loop(0, shifts, step, (zero, zero))
    inflow = jnp.dot(f_ref[...], acc_i, precision=HI, preferred_element_type=jnp.float32)
    outflow = jnp.dot(f_ref[...], acc_o, precision=HI, preferred_element_type=jnp.float32)
    occ = occ_ref[...]
    out_ref[...] = (1.0 - occ) * inflow - occ * outflow


def collide(idx, blocks, spread_w, fold, gain, loss, occ, lanes=512):
    shifts, pairs, width = gain.shape
    bands = occ.shape[0]
    sub_width = blocks.shape[2]
    sub_count = width // sub_width
    nsub = lanes // sub_width
    kern = functools.partial(collide_kernel, shifts=shifts, nsub=nsub, sub_count=sub_count, lanes=lanes)
    return pl.pallas_call(
        kern,
        out_shape=jax.ShapeDtypeStruct((bands, width), jnp.float32),
        grid_spec=pltpu.PrefetchScalarGridSpec(
            num_scalar_prefetch=1,
            grid=(width // lanes,),
            in_specs=[
                pl.BlockSpec(blocks.shape, lambda t, i: (0, 0, 0)),
                pl.BlockSpec(spread_w.shape, lambda t, i: (0, 0, 0)),
                pl.BlockSpec(fold.shape, lambda t, i: (0, 0)),
                pl.BlockSpec((shifts, pairs, lanes), lambda t, i: (0, 0, t)),
                pl.BlockSpec((shifts, pairs, lanes), lambda t, i: (0, 0, t)),
                pl.BlockSpec((bands, lanes), lambda t, i: (0, t)),
            ],
            out_specs=pl.BlockSpec((bands, lanes), lambda t, i: (0, t)),
        ),
    )(idx, blocks, spread_w, fold, gain, loss, occ)


def ring_gather(block, y_count, z_count):
    ka_count = 2 * y_count * z_count
    per_z = 2 * y_count

    def pairs(fn):
        return [(j, fn(j)) for j in range(ka_count)]

    def y_step(d):
        return pairs(lambda j: (j // per_z) * per_z + ((j // 2 + d) % y_count) * 2 + j % 2)

    def z_step(d):
        return pairs(lambda j: ((j // per_z + d) % z_count) * per_z + j % per_z)

    def ring(x, step, count):
        ahead = {0: x}
        fwd, back = x, x
        for d in range(1, count // 2 + 1):
            back = lax.ppermute(back, "ka", step(-1))
            ahead[d] = back
            if d < count - d:
                fwd = lax.ppermute(fwd, "ka", step(1))
                ahead[count - d] = fwd
        return jnp.stack([ahead[d] for d in range(count)])

    along_y = ring(block, y_step, y_count)
    along_z = ring(along_y, z_step, z_count)
    other = lax.ppermute(along_z, "ka", pairs(lambda j: j ^ 1))
    return jnp.stack([along_z, other])


def body(occupation, gain_table, loss_table, owner, local_index, pair_mask, counts):
    bands, width = occupation.shape
    shifts = gain_table.shape[0]
    sub_count = local_index.shape[3]
    sub_width = width // sub_count
    ka_count = lax.axis_size("ka")
    pb_count = lax.axis_size("pb")
    z_count = 8
    y_count = ka_count // (2 * z_count)
    total_requests = shifts * sub_count

    gathered = ring_gather(occupation, y_count, z_count).reshape(
        ka_count, bands, sub_count, sub_width
    )
    me = lax.axis_index("ka")
    my_z, my_y, my_c = me // (2 * y_count), (me // 2) % y_count, me % 2
    owners = owner.reshape(total_requests)
    o_z, o_y, o_c = owners // (2 * y_count), (owners // 2) % y_count, owners % 2
    where = (
        (o_c ^ my_c) * (z_count * y_count)
        + ((o_z - my_z) % z_count) * y_count
        + (o_y - my_y) % y_count
    )
    sources = local_index.reshape(total_requests)
    blocks = (
        gathered.transpose(0, 2, 1, 3).reshape(ka_count * sub_count, bands, sub_width)
    )
    picks = where * sub_count + sources
    active = (jnp.arange(shifts, dtype=jnp.int32) < counts.reshape(())).astype(jnp.float32)
    weight = pair_mask.astype(jnp.float32) * active[:, None]
    pair = np.arange(bands * bands)
    spread = (pair[:, None] % bands == np.arange(bands)[None, :]).astype(np.float32)
    fold = (pair[None, :] // bands == np.arange(bands)[:, None]).astype(np.float32)
    spread_w = jnp.asarray(spread)[None] * weight[:, :, None]
    partial_terms = collide(
        picks, blocks, spread_w, jnp.asarray(fold), gain_table, loss_table, occupation
    )
    share_width = width // pb_count
    parts = partial_terms.reshape(bands, pb_count, share_width).transpose(1, 0, 2)
    collision = jnp.sum(lax.all_to_all(parts, "pb", 0, 0, tiled=True), axis=0)
    own_share = lax.dynamic_slice_in_dim(
        occupation, lax.axis_index("pb") * share_width, share_width, 1
    )
    return (collision, own_share + half_step * collision)


def solution(mesh):
    return jax.shard_map(
        body,
        mesh=mesh,
        in_specs=(
            P(None, "ka"),
            P("pb", None, "ka"),
            P("pb", None, "ka"),
            P("pb", "ka", None, None, None),
            P("pb", "ka", None, None),
            P("pb", None),
            P("pb", "ka"),
        ),
        out_specs=(P(None, ("ka", "pb")), P(None, ("ka", "pb"))),
        check_vma=False,
    )
```

```python
import functools

import jax
import jax.numpy as jnp
from jax import lax
from jax.experimental import pallas as pl
from jax.experimental.pallas import tpu as pltpu
from jax.sharding import PartitionSpec as P

half_step = 0.5


def collide_kernel(idx_ref, g_ref, w_ref, gain_ref, loss_ref, occ_ref, out_ref, sh_ref, rest_ref,
                   *, shifts, nsub, sub_count, sub_width, bands):
    t = pl.program_id(0)
    for s in range(shifts):
        for jj in range(nsub):
            row = g_ref[pl.ds(idx_ref[s * sub_count + t * nsub + jj], 1), :]
            for n in range(bands):
                piece = row[:, n * sub_width:(n + 1) * sub_width]
                sh_ref[n, pl.ds(s, 1), pl.ds(jj * sub_width, sub_width)] = piece
                rest_ref[n, pl.ds(s, 1), pl.ds(jj * sub_width, sub_width)] = 1.0 - piece
    occ = occ_ref[...]
    for m in range(bands):
        acc_i = None
        acc_o = None
        for n in range(bands):
            p = m * bands + n
            w = w_ref[p]
            term_i = gain_ref[p].astype(jnp.float32) * w * sh_ref[n]
            term_o = loss_ref[p].astype(jnp.float32) * w * rest_ref[n]
            acc_i = term_i if acc_i is None else acc_i + term_i
            acc_o = term_o if acc_o is None else acc_o + term_o
        inflow = jnp.sum(acc_i, axis=0, keepdims=True)
        outflow = jnp.sum(acc_o, axis=0, keepdims=True)
        out_ref[pl.ds(m, 1), :] = (1.0 - occ[m:m + 1]) * inflow - occ[m:m + 1] * outflow


def collide(idx, rows, weight_t, gain_t, loss_t, occ, sub_width, lanes=512):
    pairs, shifts, width = gain_t.shape
    bands = occ.shape[0]
    sub_count = width // sub_width
    nsub = lanes // sub_width
    kern = functools.partial(collide_kernel, shifts=shifts, nsub=nsub, sub_count=sub_count,
                             sub_width=sub_width, bands=bands)
    return pl.pallas_call(
        kern,
        out_shape=jax.ShapeDtypeStruct((bands, width), jnp.float32),
        grid_spec=pltpu.PrefetchScalarGridSpec(
            num_scalar_prefetch=1,
            grid=(width // lanes,),
            in_specs=[
                pl.BlockSpec(rows.shape, lambda t, i: (0, 0)),
                pl.BlockSpec(weight_t.shape, lambda t, i: (0, 0, 0)),
                pl.BlockSpec((pairs, shifts, lanes), lambda t, i: (0, 0, t)),
                pl.BlockSpec((pairs, shifts, lanes), lambda t, i: (0, 0, t)),
                pl.BlockSpec((bands, lanes), lambda t, i: (0, t)),
            ],
            out_specs=pl.BlockSpec((bands, lanes), lambda t, i: (0, t)),
            scratch_shapes=[
                pltpu.VMEM((bands, shifts, lanes), jnp.float32),
                pltpu.VMEM((bands, shifts, lanes), jnp.float32),
            ],
        ),
    )(idx, rows, weight_t, gain_t, loss_t, occ)


def ring_gather(block, y_count, z_count):
    ka_count = 2 * y_count * z_count
    per_z = 2 * y_count

    def pairs(fn):
        return [(j, fn(j)) for j in range(ka_count)]

    def y_step(d):
        return pairs(lambda j: (j // per_z) * per_z + ((j // 2 + d) % y_count) * 2 + j % 2)

    def z_step(d):
        return pairs(lambda j: ((j // per_z + d) % z_count) * per_z + j % per_z)

    def ring(x, step, count):
        ahead = {0: x}
        fwd, back = x, x
        for d in range(1, count // 2 + 1):
            back = lax.ppermute(back, "ka", step(-1))
            ahead[d] = back
            if d < count - d:
                fwd = lax.ppermute(fwd, "ka", step(1))
                ahead[count - d] = fwd
        return jnp.stack([ahead[d] for d in range(count)])

    along_y = ring(block, y_step, y_count)
    along_z = ring(along_y, z_step, z_count)
    other = lax.ppermute(along_z, "ka", pairs(lambda j: j ^ 1))
    return jnp.stack([along_z, other])


def body(occupation, gain_table, loss_table, owner, local_index, pair_mask, counts):
    bands, width = occupation.shape
    shifts = gain_table.shape[0]
    sub_count = local_index.shape[3]
    sub_width = width // sub_count
    ka_count = lax.axis_size("ka")
    pb_count = lax.axis_size("pb")
    z_count = 8
    y_count = ka_count // (2 * z_count)
    total_requests = shifts * sub_count

    local_rows = (
        occupation.reshape(bands, sub_count, sub_width)
        .transpose(1, 0, 2)
        .reshape(sub_count, bands * sub_width)
    )
    rows = ring_gather(local_rows, y_count, z_count).reshape(
        ka_count * sub_count, bands * sub_width
    )
    me = lax.axis_index("ka")
    my_z, my_y, my_c = me // (2 * y_count), (me // 2) % y_count, me % 2
    owners = owner.reshape(total_requests)
    o_z, o_y, o_c = owners // (2 * y_count), (owners // 2) % y_count, owners % 2
    where = (
        (o_c ^ my_c) * (z_count * y_count)
        + ((o_z - my_z) % z_count) * y_count
        + (o_y - my_y) % y_count
    )
    sources = local_index.reshape(total_requests)
    picks = where * sub_count + sources
    active = (jnp.arange(shifts, dtype=jnp.int32) < counts.reshape(())).astype(jnp.float32)
    weight = pair_mask.astype(jnp.float32) * active[:, None]
    partial_terms = collide(
        picks,
        rows,
        weight.T[:, :, None],
        gain_table.transpose(1, 0, 2),
        loss_table.transpose(1, 0, 2),
        occupation,
        sub_width,
    )
    share_width = width // pb_count
    parts = partial_terms.reshape(bands, pb_count, share_width).transpose(1, 0, 2)
    collision = jnp.sum(lax.all_to_all(parts, "pb", 0, 0, tiled=True), axis=0)
    own_share = lax.dynamic_slice_in_dim(
        occupation, lax.axis_index("pb") * share_width, share_width, 1
    )
    return (collision, own_share + half_step * collision)


def solution(mesh):
    return jax.shard_map(
        body,
        mesh=mesh,
        in_specs=(
            P(None, "ka"),
            P("pb", None, "ka"),
            P("pb", None, "ka"),
            P("pb", "ka", None, None, None),
            P("pb", "ka", None, None),
            P("pb", None),
            P("pb", "ka"),
        ),
        out_specs=(P(None, ("ka", "pb")), P(None, ("ka", "pb"))),
        check_vma=False,
    )
```

```python
import functools

import jax
import jax.numpy as jnp
from jax import lax
from jax.experimental import pallas as pl
from jax.experimental.pallas import tpu as pltpu
from jax.sharding import PartitionSpec as P

half_step = 0.5


def collide_kernel(idx_ref, near_ref, far_ref, w_ref, gain_ref, loss_ref, occ_ref, out_ref, sh_ref, rest_ref,
                   *, shifts, nsub, sub_count, sub_width, bands):
    t = pl.program_id(0)
    half = near_ref.shape[0]
    for s in range(shifts):
        for jj in range(nsub):
            at = idx_ref[s * sub_count + t * nsub + jj]
            near = near_ref[pl.ds(jnp.minimum(at, half - 1), 1), :]
            far = far_ref[pl.ds(jnp.maximum(at - half, 0), 1), :]
            row = jnp.where(at < half, near, far)
            for n in range(bands):
                piece = row[:, n * sub_width:(n + 1) * sub_width]
                sh_ref[n, pl.ds(s, 1), pl.ds(jj * sub_width, sub_width)] = piece
                rest_ref[n, pl.ds(s, 1), pl.ds(jj * sub_width, sub_width)] = 1.0 - piece
    occ = occ_ref[...]
    for m in range(bands):
        acc_i = None
        acc_o = None
        for n in range(bands):
            p = m * bands + n
            w = w_ref[p]
            term_i = gain_ref[p].astype(jnp.float32) * w * sh_ref[n]
            term_o = loss_ref[p].astype(jnp.float32) * w * rest_ref[n]
            acc_i = term_i if acc_i is None else acc_i + term_i
            acc_o = term_o if acc_o is None else acc_o + term_o
        inflow = jnp.sum(acc_i, axis=0, keepdims=True)
        outflow = jnp.sum(acc_o, axis=0, keepdims=True)
        out_ref[pl.ds(m, 1), :] = (1.0 - occ[m:m + 1]) * inflow - occ[m:m + 1] * outflow


def collide(idx, near, far, weight_t, gain_t, loss_t, occ, sub_width, lanes=512):
    pairs, shifts, width = gain_t.shape
    bands = occ.shape[0]
    sub_count = width // sub_width
    nsub = lanes // sub_width
    kern = functools.partial(collide_kernel, shifts=shifts, nsub=nsub, sub_count=sub_count,
                             sub_width=sub_width, bands=bands)
    return pl.pallas_call(
        kern,
        out_shape=jax.ShapeDtypeStruct((bands, width), jnp.float32),
        grid_spec=pltpu.PrefetchScalarGridSpec(
            num_scalar_prefetch=1,
            grid=(width // lanes,),
            in_specs=[
                pl.BlockSpec(near.shape, lambda t, i: (0, 0)),
                pl.BlockSpec(far.shape, lambda t, i: (0, 0)),
                pl.BlockSpec(weight_t.shape, lambda t, i: (0, 0, 0)),
                pl.BlockSpec((pairs, shifts, lanes), lambda t, i: (0, 0, t)),
                pl.BlockSpec((pairs, shifts, lanes), lambda t, i: (0, 0, t)),
                pl.BlockSpec((bands, lanes), lambda t, i: (0, t)),
            ],
            out_specs=pl.BlockSpec((bands, lanes), lambda t, i: (0, t)),
            scratch_shapes=[
                pltpu.VMEM((bands, shifts, lanes), jnp.float32),
                pltpu.VMEM((bands, shifts, lanes), jnp.float32),
            ],
        ),
    )(idx, near, far, weight_t, gain_t, loss_t, occ)


def ring_gather(block, y_count, z_count):
    ka_count = 2 * y_count * z_count
    per_z = 2 * y_count

    def pairs(fn):
        return [(j, fn(j)) for j in range(ka_count)]

    def y_step(d):
        return pairs(lambda j: (j // per_z) * per_z + ((j // 2 + d) % y_count) * 2 + j % 2)

    def z_step(d):
        return pairs(lambda j: ((j // per_z + d) % z_count) * per_z + j % per_z)

    def ring(x, step, count):
        ahead = {0: x}
        fwd, back = x, x
        for d in range(1, count // 2 + 1):
            back = lax.ppermute(back, "ka", step(-1))
            ahead[d] = back
            if d < count - d:
                fwd = lax.ppermute(fwd, "ka", step(1))
                ahead[count - d] = fwd
        return jnp.stack([ahead[d] for d in range(count)])

    along_y = ring(block, y_step, y_count)
    along_z = ring(along_y, z_step, z_count)
    other = lax.ppermute(along_z, "ka", pairs(lambda j: j ^ 1))
    return along_z, other


def body(occupation, gain_table, loss_table, owner, local_index, pair_mask, counts):
    bands, width = occupation.shape
    shifts = gain_table.shape[0]
    sub_count = local_index.shape[3]
    sub_width = width // sub_count
    ka_count = lax.axis_size("ka")
    pb_count = lax.axis_size("pb")
    z_count = 8
    y_count = ka_count // (2 * z_count)
    total_requests = shifts * sub_count

    local_rows = (
        occupation.reshape(bands, sub_count, sub_width)
        .transpose(1, 0, 2)
        .reshape(sub_count, bands * sub_width)
    )
    near, far = ring_gather(local_rows, y_count, z_count)
    near = near.reshape(ka_count * sub_count // 2, bands * sub_width)
    far = far.reshape(ka_count * sub_count // 2, bands * sub_width)
    me = lax.axis_index("ka")
    my_z, my_y, my_c = me // (2 * y_count), (me // 2) % y_count, me % 2
    owners = owner.reshape(total_requests)
    o_z, o_y, o_c = owners // (2 * y_count), (owners // 2) % y_count, owners % 2
    where = (
        (o_c ^ my_c) * (z_count * y_count)
        + ((o_z - my_z) % z_count) * y_count
        + (o_y - my_y) % y_count
    )
    sources = local_index.reshape(total_requests)
    picks = where * sub_count + sources
    active = (jnp.arange(shifts, dtype=jnp.int32) < counts.reshape(())).astype(jnp.float32)
    weight = pair_mask.astype(jnp.float32) * active[:, None]
    partial_terms = collide(
        picks,
        near,
        far,
        weight.T[:, :, None],
        gain_table.transpose(1, 0, 2),
        loss_table.transpose(1, 0, 2),
        occupation,
        sub_width,
    )
    share_width = width // pb_count
    parts = partial_terms.reshape(bands, pb_count, share_width).transpose(1, 0, 2)
    collision = jnp.sum(lax.all_to_all(parts, "pb", 0, 0, tiled=True), axis=0)
    own_share = lax.dynamic_slice_in_dim(
        occupation, lax.axis_index("pb") * share_width, share_width, 1
    )
    return (collision, own_share + half_step * collision)


def solution(mesh):
    return jax.shard_map(
        body,
        mesh=mesh,
        in_specs=(
            P(None, "ka"),
            P("pb", None, "ka"),
            P("pb", None, "ka"),
            P("pb", "ka", None, None, None),
            P("pb", "ka", None, None),
            P("pb", None),
            P("pb", "ka"),
        ),
        out_specs=(P(None, ("ka", "pb")), P(None, ("ka", "pb"))),
        check_vma=False,
    )
```

```python
import functools

import jax
import jax.numpy as jnp
from jax import lax
from jax.experimental import pallas as pl
from jax.experimental.pallas import tpu as pltpu
from jax.sharding import PartitionSpec as P

half_step = 0.5


def collide_kernel(idx_ref, near_ref, far_ref, gain_ref, loss_ref, occ_ref, out_ref, sh_ref, rest_ref,
                   *, shifts, nsub, sub_count, sub_width, bands):
    t = pl.program_id(0)
    half = near_ref.shape[0]
    for s in range(shifts):
        for jj in range(nsub):
            at = idx_ref[s * sub_count + t * nsub + jj]
            near = near_ref[pl.ds(jnp.minimum(at, half - 1), 1), :]
            far = far_ref[pl.ds(jnp.maximum(at - half, 0), 1), :]
            row = jnp.where(at < half, near, far)
            for n in range(bands):
                piece = row[:, n * sub_width:(n + 1) * sub_width]
                sh_ref[n, pl.ds(s, 1), pl.ds(jj * sub_width, sub_width)] = piece
                rest_ref[n, pl.ds(s, 1), pl.ds(jj * sub_width, sub_width)] = 1.0 - piece
    occ = occ_ref[...]
    for m in range(bands):
        acc_i = None
        acc_o = None
        for n in range(bands):
            p = m * bands + n
            term_i = gain_ref[p] * sh_ref[n]
            term_o = loss_ref[p] * rest_ref[n]
            acc_i = term_i if acc_i is None else acc_i + term_i
            acc_o = term_o if acc_o is None else acc_o + term_o
        inflow = jnp.sum(acc_i, axis=0, keepdims=True)
        outflow = jnp.sum(acc_o, axis=0, keepdims=True)
        out_ref[pl.ds(m, 1), :] = (1.0 - occ[m:m + 1]) * inflow - occ[m:m + 1] * outflow


def collide(idx, near, far, gain_t, loss_t, occ, sub_width, lanes=512):
    pairs, shifts, width = gain_t.shape
    bands = occ.shape[0]
    sub_count = width // sub_width
    nsub = lanes // sub_width
    kern = functools.partial(collide_kernel, shifts=shifts, nsub=nsub, sub_count=sub_count,
                             sub_width=sub_width, bands=bands)
    return pl.pallas_call(
        kern,
        out_shape=jax.ShapeDtypeStruct((bands, width), jnp.float32),
        grid_spec=pltpu.PrefetchScalarGridSpec(
            num_scalar_prefetch=1,
            grid=(width // lanes,),
            in_specs=[
                pl.BlockSpec(near.shape, lambda t, i: (0, 0)),
                pl.BlockSpec(far.shape, lambda t, i: (0, 0)),
                pl.BlockSpec((pairs, shifts, lanes), lambda t, i: (0, 0, t)),
                pl.BlockSpec((pairs, shifts, lanes), lambda t, i: (0, 0, t)),
                pl.BlockSpec((bands, lanes), lambda t, i: (0, t)),
            ],
            out_specs=pl.BlockSpec((bands, lanes), lambda t, i: (0, t)),
            scratch_shapes=[
                pltpu.VMEM((bands, shifts, lanes), jnp.float32),
                pltpu.VMEM((bands, shifts, lanes), jnp.float32),
            ],
        ),
    )(idx, near, far, gain_t, loss_t, occ)


def ring_gather(block, y_count, z_count, riders):
    ka_count = 2 * y_count * z_count
    per_z = 2 * y_count

    def pairs(fn):
        return [(j, fn(j)) for j in range(ka_count)]

    def y_step(d):
        return pairs(lambda j: (j // per_z) * per_z + ((j // 2 + d) % y_count) * 2 + j % 2)

    def z_step(d):
        return pairs(lambda j: ((j // per_z + d) % z_count) * per_z + j % per_z)

    def ring(x, step, count):
        ahead = {0: x}
        fwd, back = x, x
        for d in range(1, count // 2 + 1):
            back = lax.ppermute(back, "ka", step(-1))
            ahead[d] = back
            if d < count - d:
                fwd = lax.ppermute(fwd, "ka", step(1))
                ahead[count - d] = fwd
        return jnp.stack([ahead[d] for d in range(count)])

    along_y = ring(block, y_step, y_count)
    along_y, riders = lax.optimization_barrier((along_y, riders))
    along_z = ring(along_y, z_step, z_count)
    other = lax.ppermute(along_z, "ka", pairs(lambda j: j ^ 1))
    return along_z, other, riders


def body(occupation, gain_table, loss_table, owner, local_index, pair_mask, counts):
    bands, width = occupation.shape
    shifts = gain_table.shape[0]
    sub_count = local_index.shape[3]
    sub_width = width // sub_count
    ka_count = lax.axis_size("ka")
    pb_count = lax.axis_size("pb")
    z_count = 8
    y_count = ka_count // (2 * z_count)
    total_requests = shifts * sub_count

    local_rows = (
        occupation.reshape(bands, sub_count, sub_width)
        .transpose(1, 0, 2)
        .reshape(sub_count, bands * sub_width)
    )
    active = (jnp.arange(shifts, dtype=jnp.int32) < counts.reshape(())).astype(jnp.float32)
    weight_t = (pair_mask.astype(jnp.float32) * active[:, None]).T[:, :, None]
    gain_w = gain_table.transpose(1, 0, 2).astype(jnp.float32) * weight_t
    loss_w = loss_table.transpose(1, 0, 2).astype(jnp.float32) * weight_t
    near, far, (gain_w, loss_w) = ring_gather(local_rows, y_count, z_count, (gain_w, loss_w))
    near = near.reshape(ka_count * sub_count // 2, bands * sub_width)
    far = far.reshape(ka_count * sub_count // 2, bands * sub_width)
    me = lax.axis_index("ka")
    my_z, my_y, my_c = me // (2 * y_count), (me // 2) % y_count, me % 2
    owners = owner.reshape(total_requests)
    o_z, o_y, o_c = owners // (2 * y_count), (owners // 2) % y_count, owners % 2
    where = (
        (o_c ^ my_c) * (z_count * y_count)
        + ((o_z - my_z) % z_count) * y_count
        + (o_y - my_y) % y_count
    )
    sources = local_index.reshape(total_requests)
    picks = where * sub_count + sources
    partial_terms = collide(
        picks,
        near,
        far,
        gain_w,
        loss_w,
        occupation,
        sub_width,
    )
    share_width = width // pb_count
    parts = partial_terms.reshape(bands, pb_count, share_width).transpose(1, 0, 2)
    collision = jnp.sum(lax.all_to_all(parts, "pb", 0, 0, tiled=True), axis=0)
    own_share = lax.dynamic_slice_in_dim(
        occupation, lax.axis_index("pb") * share_width, share_width, 1
    )
    return (collision, own_share + half_step * collision)


def solution(mesh):
    return jax.shard_map(
        body,
        mesh=mesh,
        in_specs=(
            P(None, "ka"),
            P("pb", None, "ka"),
            P("pb", None, "ka"),
            P("pb", "ka", None, None, None),
            P("pb", "ka", None, None),
            P("pb", None),
            P("pb", "ka"),
        ),
        out_specs=(P(None, ("ka", "pb")), P(None, ("ka", "pb"))),
        check_vma=False,
    )
```

```python
import functools

import jax
import jax.numpy as jnp
from jax import lax
from jax.experimental import pallas as pl
from jax.experimental.pallas import tpu as pltpu
from jax.sharding import PartitionSpec as P

half_step = 0.5


def collide_kernel(idx_ref, a_ref, b_ref, c_ref, d_ref, w_ref, gain_ref, loss_ref, occ_ref, out_ref, sh_ref, rest_ref,
                   *, shifts, nsub, sub_count, sub_width, bands):
    t = pl.program_id(0)
    quarter = a_ref.shape[0]
    for s in range(shifts):
        for jj in range(nsub):
            at = idx_ref[s * sub_count + t * nsub + jj]
            part = at // quarter
            off = at % quarter
            row = jnp.where(
                part < 2,
                jnp.where(part == 0, a_ref[pl.ds(off, 1), :], b_ref[pl.ds(off, 1), :]),
                jnp.where(part == 2, c_ref[pl.ds(off, 1), :], d_ref[pl.ds(off, 1), :]),
            )
            for n in range(bands):
                piece = row[:, n * sub_width:(n + 1) * sub_width]
                sh_ref[n, pl.ds(s, 1), pl.ds(jj * sub_width, sub_width)] = piece
                rest_ref[n, pl.ds(s, 1), pl.ds(jj * sub_width, sub_width)] = 1.0 - piece
    occ = occ_ref[...]
    for m in range(bands):
        acc_i = None
        acc_o = None
        for n in range(bands):
            p = m * bands + n
            w = w_ref[p]
            term_i = gain_ref[p].astype(jnp.float32) * w * sh_ref[n]
            term_o = loss_ref[p].astype(jnp.float32) * w * rest_ref[n]
            acc_i = term_i if acc_i is None else acc_i + term_i
            acc_o = term_o if acc_o is None else acc_o + term_o
        inflow = jnp.sum(acc_i, axis=0, keepdims=True)
        outflow = jnp.sum(acc_o, axis=0, keepdims=True)
        out_ref[pl.ds(m, 1), :] = (1.0 - occ[m:m + 1]) * inflow - occ[m:m + 1] * outflow


def collide(idx, quads, weight_t, gain_t, loss_t, occ, sub_width, lanes=512):
    pairs, shifts, width = gain_t.shape
    bands = occ.shape[0]
    sub_count = width // sub_width
    nsub = lanes // sub_width
    kern = functools.partial(collide_kernel, shifts=shifts, nsub=nsub, sub_count=sub_count,
                             sub_width=sub_width, bands=bands)
    return pl.pallas_call(
        kern,
        out_shape=jax.ShapeDtypeStruct((bands, width), jnp.float32),
        grid_spec=pltpu.PrefetchScalarGridSpec(
            num_scalar_prefetch=1,
            grid=(width // lanes,),
            in_specs=[
                *[pl.BlockSpec(q.shape, lambda t, i: (0, 0)) for q in quads],
                pl.BlockSpec(weight_t.shape, lambda t, i: (0, 0, 0)),
                pl.BlockSpec((pairs, shifts, lanes), lambda t, i: (0, 0, t)),
                pl.BlockSpec((pairs, shifts, lanes), lambda t, i: (0, 0, t)),
                pl.BlockSpec((bands, lanes), lambda t, i: (0, t)),
            ],
            out_specs=pl.BlockSpec((bands, lanes), lambda t, i: (0, t)),
            scratch_shapes=[
                pltpu.VMEM((bands, shifts, lanes), jnp.float32),
                pltpu.VMEM((bands, shifts, lanes), jnp.float32),
            ],
        ),
    )(idx, *quads, weight_t, gain_t, loss_t, occ)


def ring_gather(block, y_count, z_count):
    ka_count = 2 * y_count * z_count
    per_z = 2 * y_count

    def pairs(fn):
        return [(j, fn(j)) for j in range(ka_count)]

    def y_step(d):
        return pairs(lambda j: (j // per_z) * per_z + ((j // 2 + d) % y_count) * 2 + j % 2)

    def z_step(d):
        return pairs(lambda j: ((j // per_z + d) % z_count) * per_z + j % per_z)

    def ring(x, step, count):
        ahead = {0: x}
        fwd, back = x, x
        for d in range(1, count // 2 + 1):
            back = lax.ppermute(back, "ka", step(-1))
            ahead[d] = back
            if d < count - d:
                fwd = lax.ppermute(fwd, "ka", step(1))
                ahead[count - d] = fwd
        return jnp.stack([ahead[d] for d in range(count)])

    half = block.shape[0] // 2
    first, second = block[:half], block[half:]
    first_y = ring(first, y_step, y_count)
    second_z = ring(second, z_step, z_count)
    first_yz = ring(first_y, z_step, z_count)
    second_zy = ring(second_z, y_step, y_count)
    swap = pairs(lambda j: j ^ 1)
    return (
        first_yz,
        lax.ppermute(first_yz, "ka", swap),
        second_zy,
        lax.ppermute(second_zy, "ka", swap),
    )


def body(occupation, gain_table, loss_table, owner, local_index, pair_mask, counts):
    bands, width = occupation.shape
    shifts = gain_table.shape[0]
    sub_count = local_index.shape[3]
    sub_width = width // sub_count
    ka_count = lax.axis_size("ka")
    pb_count = lax.axis_size("pb")
    z_count = 8
    y_count = ka_count // (2 * z_count)
    total_requests = shifts * sub_count

    local_rows = (
        occupation.reshape(bands, sub_count, sub_width)
        .transpose(1, 0, 2)
        .reshape(sub_count, bands * sub_width)
    )
    quads = [
        q.reshape(ka_count * sub_count // 4, bands * sub_width)
        for q in ring_gather(local_rows, y_count, z_count)
    ]
    me = lax.axis_index("ka")
    my_z, my_y, my_c = me // (2 * y_count), (me // 2) % y_count, me % 2
    owners = owner.reshape(total_requests)
    o_z, o_y, o_c = owners // (2 * y_count), (owners // 2) % y_count, owners % 2
    sources = local_index.reshape(total_requests)
    half_sub = sub_count // 2
    core_off = o_c ^ my_c
    dz = (o_z - my_z) % z_count
    dy = (o_y - my_y) % y_count
    low = sources < half_sub
    picks = jnp.where(
        low,
        ((core_off * z_count + dz) * y_count + dy) * half_sub + sources,
        ka_count * half_sub
        + ((core_off * y_count + dy) * z_count + dz) * half_sub
        + sources
        - half_sub,
    )
    active = (jnp.arange(shifts, dtype=jnp.int32) < counts.reshape(())).astype(jnp.float32)
    weight = pair_mask.astype(jnp.float32) * active[:, None]
    partial_terms = collide(
        picks,
        quads,
        weight.T[:, :, None],
        gain_table.transpose(1, 0, 2),
        loss_table.transpose(1, 0, 2),
        occupation,
        sub_width,
    )
    share_width = width // pb_count
    parts = partial_terms.reshape(bands, pb_count, share_width).transpose(1, 0, 2)
    collision = jnp.sum(lax.all_to_all(parts, "pb", 0, 0, tiled=True), axis=0)
    own_share = lax.dynamic_slice_in_dim(
        occupation, lax.axis_index("pb") * share_width, share_width, 1
    )
    return (collision, own_share + half_step * collision)


def solution(mesh):
    return jax.shard_map(
        body,
        mesh=mesh,
        in_specs=(
            P(None, "ka"),
            P("pb", None, "ka"),
            P("pb", None, "ka"),
            P("pb", "ka", None, None, None),
            P("pb", "ka", None, None),
            P("pb", None),
            P("pb", "ka"),
        ),
        out_specs=(P(None, ("ka", "pb")), P(None, ("ka", "pb"))),
        check_vma=False,
    )
```

```python
import functools

import jax
import jax.numpy as jnp
from jax import lax
from jax.experimental import pallas as pl
from jax.experimental.pallas import tpu as pltpu
from jax.sharding import PartitionSpec as P

half_step = 0.5


def collide_kernel(idx_ref, tiles_ref, near_ref, far_ref, w_ref, gain_ref, loss_ref, occ_ref, out_ref, sh_ref, rest_ref,
                   *, shifts, nsub, sub_count, sub_width, bands):
    tile = tiles_ref[pl.program_id(0)]
    half = near_ref.shape[0]
    for s in range(shifts):
        for jj in range(nsub):
            at = idx_ref[s * sub_count + tile * nsub + jj]
            near = near_ref[pl.ds(jnp.minimum(at, half - 1), 1), :]
            far = far_ref[pl.ds(jnp.maximum(at - half, 0), 1), :]
            row = jnp.where(at < half, near, far)
            for n in range(bands):
                piece = row[:, n * sub_width:(n + 1) * sub_width]
                sh_ref[n, pl.ds(s, 1), pl.ds(jj * sub_width, sub_width)] = piece
                rest_ref[n, pl.ds(s, 1), pl.ds(jj * sub_width, sub_width)] = 1.0 - piece
    occ = occ_ref[...]
    for m in range(bands):
        acc_i = None
        acc_o = None
        for n in range(bands):
            p = m * bands + n
            w = w_ref[p]
            term_i = gain_ref[p].astype(jnp.float32) * w * sh_ref[n]
            term_o = loss_ref[p].astype(jnp.float32) * w * rest_ref[n]
            acc_i = term_i if acc_i is None else acc_i + term_i
            acc_o = term_o if acc_o is None else acc_o + term_o
        inflow = jnp.sum(acc_i, axis=0, keepdims=True)
        outflow = jnp.sum(acc_o, axis=0, keepdims=True)
        out_ref[pl.ds(m, 1), :] = (1.0 - occ[m:m + 1]) * inflow - occ[m:m + 1] * outflow


def collide(idx, tiles, near, far, weight_t, gain_t, loss_t, occ, sub_width, lanes):
    pairs, shifts, width = gain_t.shape
    count = tiles.shape[0]
    bands = occ.shape[0]
    sub_count = width // sub_width
    nsub = lanes // sub_width
    kern = functools.partial(collide_kernel, shifts=shifts, nsub=nsub, sub_count=sub_count,
                             sub_width=sub_width, bands=bands)
    return pl.pallas_call(
        kern,
        out_shape=jax.ShapeDtypeStruct((bands, count * lanes), jnp.float32),
        grid_spec=pltpu.PrefetchScalarGridSpec(
            num_scalar_prefetch=2,
            grid=(count,),
            in_specs=[
                pl.BlockSpec(near.shape, lambda t, i, c: (0, 0)),
                pl.BlockSpec(far.shape, lambda t, i, c: (0, 0)),
                pl.BlockSpec(weight_t.shape, lambda t, i, c: (0, 0, 0)),
                pl.BlockSpec((pairs, shifts, lanes), lambda t, i, c: (0, 0, c[t])),
                pl.BlockSpec((pairs, shifts, lanes), lambda t, i, c: (0, 0, c[t])),
                pl.BlockSpec((bands, lanes), lambda t, i, c: (0, c[t])),
            ],
            out_specs=pl.BlockSpec((bands, lanes), lambda t, i, c: (0, t)),
            scratch_shapes=[
                pltpu.VMEM((bands, shifts, lanes), jnp.float32),
                pltpu.VMEM((bands, shifts, lanes), jnp.float32),
            ],
        ),
    )(idx, tiles, near, far, weight_t, gain_t, loss_t, occ)


def ring_gather(block, y_count, z_count):
    ka_count = 2 * y_count * z_count
    per_z = 2 * y_count

    def pairs(fn):
        return [(j, fn(j)) for j in range(ka_count)]

    def y_step(d):
        return pairs(lambda j: (j // per_z) * per_z + ((j // 2 + d) % y_count) * 2 + j % 2)

    def z_step(d):
        return pairs(lambda j: ((j // per_z + d) % z_count) * per_z + j % per_z)

    def ring(x, step, count):
        ahead = {0: x}
        fwd, back = x, x
        for d in range(1, count // 2 + 1):
            back = lax.ppermute(back, "ka", step(-1))
            ahead[d] = back
            if d < count - d:
                fwd = lax.ppermute(fwd, "ka", step(1))
                ahead[count - d] = fwd
        return jnp.stack([ahead[d] for d in range(count)])

    along_y = ring(block, y_step, y_count)
    along_z = ring(along_y, z_step, z_count)
    other = lax.ppermute(along_z, "ka", pairs(lambda j: j ^ 1))
    return along_z, other


def body(occupation, gain_table, loss_table, owner, local_index, pair_mask, counts):
    bands, width = occupation.shape
    shifts = gain_table.shape[0]
    sub_count = local_index.shape[3]
    sub_width = width // sub_count
    ka_count = lax.axis_size("ka")
    pb_count = lax.axis_size("pb")
    z_count = 8
    y_count = ka_count // (2 * z_count)
    total_requests = shifts * sub_count

    local_rows = (
        occupation.reshape(bands, sub_count, sub_width)
        .transpose(1, 0, 2)
        .reshape(sub_count, bands * sub_width)
    )
    near, far = ring_gather(local_rows, y_count, z_count)
    near = near.reshape(ka_count * sub_count // 2, bands * sub_width)
    far = far.reshape(ka_count * sub_count // 2, bands * sub_width)
    me = lax.axis_index("ka")
    my_z, my_y, my_c = me // (2 * y_count), (me // 2) % y_count, me % 2
    owners = owner.reshape(total_requests)
    o_z, o_y, o_c = owners // (2 * y_count), (owners // 2) % y_count, owners % 2
    where = (
        (o_c ^ my_c) * (z_count * y_count)
        + ((o_z - my_z) % z_count) * y_count
        + (o_y - my_y) % y_count
    )
    sources = local_index.reshape(total_requests)
    picks = where * sub_count + sources
    active = (jnp.arange(shifts, dtype=jnp.int32) < counts.reshape(())).astype(jnp.float32)
    weight = pair_mask.astype(jnp.float32) * active[:, None]
    lanes = 512
    share_width = width // pb_count
    per_share = share_width // lanes
    me_pb = lax.axis_index("pb")
    step = jnp.arange(per_share, dtype=jnp.int32)
    remote = jnp.concatenate(
        [((me_pb + d) % pb_count) * per_share + step for d in range(1, pb_count)]
    )
    own = me_pb * per_share + step
    tables = (picks, near, far, weight.T[:, :, None],
              gain_table.transpose(1, 0, 2), loss_table.transpose(1, 0, 2), occupation)
    sent = collide(tables[0], remote, *tables[1:], sub_width, lanes)
    slots = jnp.concatenate([jnp.zeros((bands, share_width), jnp.float32), sent], axis=1)
    slots = slots.reshape(bands, pb_count, share_width).transpose(1, 0, 2)
    by_target = lax.dynamic_slice_in_dim(
        jnp.concatenate([slots, slots]), (pb_count - me_pb) % pb_count, pb_count, 0
    )
    received = lax.all_to_all(by_target, "pb", 0, 0, tiled=True)
    kept = collide(tables[0], own, *tables[1:], sub_width, lanes)
    collision = kept + jnp.sum(received, axis=0)
    own_share = lax.dynamic_slice_in_dim(
        occupation, lax.axis_index("pb") * share_width, share_width, 1
    )
    return (collision, own_share + half_step * collision)


def solution(mesh):
    return jax.shard_map(
        body,
        mesh=mesh,
        in_specs=(
            P(None, "ka"),
            P("pb", None, "ka"),
            P("pb", None, "ka"),
            P("pb", "ka", None, None, None),
            P("pb", "ka", None, None),
            P("pb", None),
            P("pb", "ka"),
        ),
        out_specs=(P(None, ("ka", "pb")), P(None, ("ka", "pb"))),
        check_vma=False,
    )
```

```python
import functools

import jax
import jax.numpy as jnp
from jax import lax
from jax.experimental import pallas as pl
from jax.experimental.pallas import tpu as pltpu
from jax.sharding import PartitionSpec as P

half_step = 0.5


def collide_kernel(idx_ref, near_ref, far_ref, w_ref, gain_ref, loss_ref, occ_ref, out_ref, sh_ref, rest_ref,
                   *, shifts, nsub, sub_count, sub_width, bands):
    t = pl.program_id(0)
    half = near_ref.shape[0]
    for s in range(shifts):
        for jj in range(nsub):
            at = idx_ref[s * sub_count + t * nsub + jj]
            near = near_ref[pl.ds(jnp.minimum(at, half - 1), 1), :]
            far = far_ref[pl.ds(jnp.maximum(at - half, 0), 1), :]
            row = jnp.where(at < half, near, far)
            for n in range(bands):
                piece = row[:, n * sub_width:(n + 1) * sub_width]
                sh_ref[n, pl.ds(s, 1), pl.ds(jj * sub_width, sub_width)] = piece
    for n in range(bands):
        rest_ref[n] = 1.0 - sh_ref[n]
    occ = occ_ref[...]
    for m in range(bands):
        acc_i = None
        acc_o = None
        for n in range(bands):
            p = m * bands + n
            w = jnp.tile(w_ref[p], (1, gain_ref.shape[2] // w_ref.shape[2]))
            term_i = gain_ref[p].astype(jnp.float32) * w * sh_ref[n]
            term_o = loss_ref[p].astype(jnp.float32) * w * rest_ref[n]
            acc_i = term_i if acc_i is None else acc_i + term_i
            acc_o = term_o if acc_o is None else acc_o + term_o
        inflow = jnp.sum(acc_i, axis=0, keepdims=True)
        outflow = jnp.sum(acc_o, axis=0, keepdims=True)
        out_ref[pl.ds(m, 1), :] = (1.0 - occ[m:m + 1]) * inflow - occ[m:m + 1] * outflow


def collide(idx, near, far, weight_t, gain_t, loss_t, occ, sub_width, lanes=1024):
    pairs, shifts, width = gain_t.shape
    bands = occ.shape[0]
    sub_count = width // sub_width
    nsub = lanes // sub_width
    kern = functools.partial(collide_kernel, shifts=shifts, nsub=nsub, sub_count=sub_count,
                             sub_width=sub_width, bands=bands)
    return pl.pallas_call(
        kern,
        out_shape=jax.ShapeDtypeStruct((bands, width), jnp.float32),
        grid_spec=pltpu.PrefetchScalarGridSpec(
            num_scalar_prefetch=1,
            grid=(width // lanes,),
            in_specs=[
                pl.BlockSpec(near.shape, lambda t, i: (0, 0)),
                pl.BlockSpec(far.shape, lambda t, i: (0, 0)),
                pl.BlockSpec(weight_t.shape, lambda t, i: (0, 0, 0)),
                pl.BlockSpec((pairs, shifts, lanes), lambda t, i: (0, 0, t)),
                pl.BlockSpec((pairs, shifts, lanes), lambda t, i: (0, 0, t)),
                pl.BlockSpec((bands, lanes), lambda t, i: (0, t)),
            ],
            out_specs=pl.BlockSpec((bands, lanes), lambda t, i: (0, t)),
            scratch_shapes=[
                pltpu.VMEM((bands, shifts, lanes), jnp.float32),
                pltpu.VMEM((bands, shifts, lanes), jnp.float32),
            ],
        ),
    )(idx, near, far, weight_t, gain_t, loss_t, occ)


def ring_gather(block, y_count, z_count):
    ka_count = 2 * y_count * z_count
    per_z = 2 * y_count

    def pairs(fn):
        return [(j, fn(j)) for j in range(ka_count)]

    def y_step(d):
        return pairs(lambda j: (j // per_z) * per_z + ((j // 2 + d) % y_count) * 2 + j % 2)

    def z_step(d):
        return pairs(lambda j: ((j // per_z + d) % z_count) * per_z + j % per_z)

    def ring(x, step, count):
        ahead = {0: x}
        fwd, back = x, x
        for d in range(1, count // 2 + 1):
            back = lax.ppermute(back, "ka", step(-1))
            ahead[d] = back
            if d < count - d:
                fwd = lax.ppermute(fwd, "ka", step(1))
                ahead[count - d] = fwd
        return jnp.stack([ahead[d] for d in range(count)])

    along_y = ring(block, y_step, y_count)
    along_z = ring(along_y, z_step, z_count)
    other = lax.ppermute(along_z, "ka", pairs(lambda j: j ^ 1))
    return along_z, other


def body(occupation, gain_table, loss_table, owner, local_index, pair_mask, counts):
    bands, width = occupation.shape
    shifts = gain_table.shape[0]
    sub_count = local_index.shape[3]
    sub_width = width // sub_count
    ka_count = lax.axis_size("ka")
    pb_count = lax.axis_size("pb")
    z_count = 8
    y_count = ka_count // (2 * z_count)
    total_requests = shifts * sub_count

    local_rows = (
        occupation.reshape(bands, sub_count, sub_width)
        .transpose(1, 0, 2)
        .reshape(sub_count, bands * sub_width)
    )
    near, far = ring_gather(local_rows, y_count, z_count)
    near = near.reshape(ka_count * sub_count // 2, bands * sub_width)
    far = far.reshape(ka_count * sub_count // 2, bands * sub_width)
    me = lax.axis_index("ka")
    my_z, my_y, my_c = me // (2 * y_count), (me // 2) % y_count, me % 2
    owners = owner.reshape(total_requests)
    o_z, o_y, o_c = owners // (2 * y_count), (owners // 2) % y_count, owners % 2
    where = (
        (o_c ^ my_c) * (z_count * y_count)
        + ((o_z - my_z) % z_count) * y_count
        + (o_y - my_y) % y_count
    )
    sources = local_index.reshape(total_requests)
    picks = where * sub_count + sources
    active = (jnp.arange(shifts, dtype=jnp.int32) < counts.reshape(())).astype(jnp.float32)
    weight = pair_mask.astype(jnp.float32) * active[:, None]
    partial_terms = collide(
        picks,
        near,
        far,
        jnp.broadcast_to(weight.T[:, :, None], (bands * bands, shifts, sub_width)),
        gain_table.transpose(1, 0, 2),
        loss_table.transpose(1, 0, 2),
        occupation,
        sub_width,
    )
    share_width = width // pb_count
    parts = partial_terms.reshape(bands, pb_count, share_width).transpose(1, 0, 2)
    collision = jnp.sum(lax.all_to_all(parts, "pb", 0, 0, tiled=True), axis=0)
    own_share = lax.dynamic_slice_in_dim(
        occupation, lax.axis_index("pb") * share_width, share_width, 1
    )
    return (collision, own_share + half_step * collision)


def solution(mesh):
    return jax.shard_map(
        body,
        mesh=mesh,
        in_specs=(
            P(None, "ka"),
            P("pb", None, "ka"),
            P("pb", None, "ka"),
            P("pb", "ka", None, None, None),
            P("pb", "ka", None, None),
            P("pb", None),
            P("pb", "ka"),
        ),
        out_specs=(P(None, ("ka", "pb")), P(None, ("ka", "pb"))),
        check_vma=False,
    )
```

```python
import functools

import jax
import jax.numpy as jnp
from jax import lax
from jax.experimental import pallas as pl
from jax.experimental.pallas import tpu as pltpu
from jax.sharding import PartitionSpec as P

half_step = 0.5


def collide_kernel(idx_ref, near_ref, far_ref, w_ref, gain_ref, loss_ref, occ_ref, out_ref, sh_ref, rest_ref,
                   *, shifts, nsub, sub_count, sub_width, bands):
    t = pl.program_id(0)
    half = near_ref.shape[0]
    for s in range(shifts):
        for jj in range(nsub):
            at = idx_ref[s * sub_count + t * nsub + jj]
            near = near_ref[pl.ds(jnp.minimum(at, half - 1), 1), :]
            far = far_ref[pl.ds(jnp.maximum(at - half, 0), 1), :]
            row = jnp.where(at < half, near, far)
            for n in range(bands):
                piece = row[:, n * sub_width:(n + 1) * sub_width]
                sh_ref[n, pl.ds(s, 1), pl.ds(jj * sub_width, sub_width)] = piece
    for n in range(bands):
        rest_ref[n] = 1.0 - sh_ref[n]
    occ = occ_ref[...]
    for m in range(bands):
        acc_i = None
        acc_o = None
        for n in range(bands):
            p = m * bands + n
            w = jnp.tile(w_ref[p], (1, gain_ref.shape[2] // w_ref.shape[2]))
            term_i = gain_ref[p].astype(jnp.float32) * w * sh_ref[n]
            term_o = loss_ref[p].astype(jnp.float32) * w * rest_ref[n]
            acc_i = term_i if acc_i is None else acc_i + term_i
            acc_o = term_o if acc_o is None else acc_o + term_o
        inflow = jnp.sum(acc_i, axis=0, keepdims=True)
        outflow = jnp.sum(acc_o, axis=0, keepdims=True)
        out_ref[pl.ds(m, 1), :] = (1.0 - occ[m:m + 1]) * inflow - occ[m:m + 1] * outflow


def collide(idx, near, far, weight_t, gain_t, loss_t, occ, sub_width, lanes=1024):
    pairs, shifts, width = gain_t.shape
    bands = occ.shape[0]
    sub_count = width // sub_width
    nsub = lanes // sub_width
    kern = functools.partial(collide_kernel, shifts=shifts, nsub=nsub, sub_count=sub_count,
                             sub_width=sub_width, bands=bands)
    return pl.pallas_call(
        kern,
        out_shape=jax.ShapeDtypeStruct((bands, width), jnp.float32),
        grid_spec=pltpu.PrefetchScalarGridSpec(
            num_scalar_prefetch=1,
            grid=(width // lanes,),
            in_specs=[
                pl.BlockSpec(near.shape, lambda t, i: (0, 0)),
                pl.BlockSpec(far.shape, lambda t, i: (0, 0)),
                pl.BlockSpec(weight_t.shape, lambda t, i: (0, 0, 0)),
                pl.BlockSpec((pairs, shifts, lanes), lambda t, i: (0, 0, t)),
                pl.BlockSpec((pairs, shifts, lanes), lambda t, i: (0, 0, t)),
                pl.BlockSpec((bands, lanes), lambda t, i: (0, t)),
            ],
            out_specs=pl.BlockSpec((bands, lanes), lambda t, i: (0, t)),
            scratch_shapes=[
                pltpu.VMEM((bands, shifts, lanes), jnp.float32),
                pltpu.VMEM((bands, shifts, lanes), jnp.float32),
            ],
        ),
    )(idx, near, far, weight_t, gain_t, loss_t, occ)


def ring_gather(block, y_count, z_count):
    ka_count = 2 * y_count * z_count
    per_z = 2 * y_count

    def pairs(fn):
        return [(j, fn(j)) for j in range(ka_count)]

    def y_step(d):
        return pairs(lambda j: (j // per_z) * per_z + ((j // 2 + d) % y_count) * 2 + j % 2)

    def z_step(d):
        return pairs(lambda j: ((j // per_z + d) % z_count) * per_z + j % per_z)

    def ring(x, step, count):
        ahead = {0: x}
        fwd, back = x, x
        for d in range(1, count // 2 + 1):
            if d < count - d:
                back = lax.ppermute(back, "ka", step(-1))
                fwd = lax.ppermute(fwd, "ka", step(1))
                ahead[d] = back
                ahead[count - d] = fwd
            else:
                cut = x.shape[0] // 2
                low = lax.ppermute(back[:cut], "ka", step(-1))
                high = lax.ppermute(fwd[cut:], "ka", step(1))
                ahead[d] = jnp.concatenate([low, high])
        return jnp.stack([ahead[d] for d in range(count)])

    along_y = ring(block, y_step, y_count)
    along_z = ring(along_y, z_step, z_count)
    other = lax.ppermute(along_z, "ka", pairs(lambda j: j ^ 1))
    return along_z, other


def body(occupation, gain_table, loss_table, owner, local_index, pair_mask, counts):
    bands, width = occupation.shape
    shifts = gain_table.shape[0]
    sub_count = local_index.shape[3]
    sub_width = width // sub_count
    ka_count = lax.axis_size("ka")
    pb_count = lax.axis_size("pb")
    z_count = 8
    y_count = ka_count // (2 * z_count)
    total_requests = shifts * sub_count

    local_rows = (
        occupation.reshape(bands, sub_count, sub_width)
        .transpose(1, 0, 2)
        .reshape(sub_count, bands * sub_width)
    )
    near, far = ring_gather(local_rows, y_count, z_count)
    near = near.reshape(ka_count * sub_count // 2, bands * sub_width)
    far = far.reshape(ka_count * sub_count // 2, bands * sub_width)
    me = lax.axis_index("ka")
    my_z, my_y, my_c = me // (2 * y_count), (me // 2) % y_count, me % 2
    owners = owner.reshape(total_requests)
    o_z, o_y, o_c = owners // (2 * y_count), (owners // 2) % y_count, owners % 2
    where = (
        (o_c ^ my_c) * (z_count * y_count)
        + ((o_z - my_z) % z_count) * y_count
        + (o_y - my_y) % y_count
    )
    sources = local_index.reshape(total_requests)
    picks = where * sub_count + sources
    active = (jnp.arange(shifts, dtype=jnp.int32) < counts.reshape(())).astype(jnp.float32)
    weight = pair_mask.astype(jnp.float32) * active[:, None]
    partial_terms = collide(
        picks,
        near,
        far,
        jnp.broadcast_to(weight.T[:, :, None], (bands * bands, shifts, sub_width)),
        gain_table.transpose(1, 0, 2),
        loss_table.transpose(1, 0, 2),
        occupation,
        sub_width,
    )
    share_width = width // pb_count
    parts = partial_terms.reshape(bands, pb_count, share_width).transpose(1, 0, 2)
    collision = jnp.sum(lax.all_to_all(parts, "pb", 0, 0, tiled=True), axis=0)
    own_share = lax.dynamic_slice_in_dim(
        occupation, lax.axis_index("pb") * share_width, share_width, 1
    )
    return (collision, own_share + half_step * collision)


def solution(mesh):
    return jax.shard_map(
        body,
        mesh=mesh,
        in_specs=(
            P(None, "ka"),
            P("pb", None, "ka"),
            P("pb", None, "ka"),
            P("pb", "ka", None, None, None),
            P("pb", "ka", None, None),
            P("pb", None),
            P("pb", "ka"),
        ),
        out_specs=(P(None, ("ka", "pb")), P(None, ("ka", "pb"))),
        check_vma=False,
    )
```

```python
import functools

import jax
import jax.numpy as jnp
from jax import lax
from jax.experimental import pallas as pl
from jax.experimental.pallas import tpu as pltpu
from jax.sharding import PartitionSpec as P

half_step = 0.5


def collide_kernel(idx_ref, near_ref, far_ref, w_ref, gain_ref, loss_ref, occ_ref, out_ref, sh_ref, rest_ref,
                   *, shifts, nsub, sub_count, sub_width, bands):
    t = pl.program_id(0)
    half = near_ref.shape[0]
    for s in range(shifts):
        for jj in range(nsub):
            at = idx_ref[s * sub_count + t * nsub + jj]
            near = near_ref[pl.ds(jnp.minimum(at, half - 1), 1), :]
            far = far_ref[pl.ds(jnp.maximum(at - half, 0), 1), :]
            row = jnp.where(at < half, near, far)
            for n in range(bands):
                piece = row[:, n * sub_width:(n + 1) * sub_width]
                sh_ref[n, pl.ds(s, 1), pl.ds(jj * sub_width, sub_width)] = piece
    for n in range(bands):
        rest_ref[n] = 1.0 - sh_ref[n]
    occ = occ_ref[...]
    for m in range(bands):
        acc_i = None
        acc_o = None
        for n in range(bands):
            p = m * bands + n
            w = jnp.tile(w_ref[p], (1, gain_ref.shape[2] // w_ref.shape[2]))
            term_i = gain_ref[p].astype(jnp.float32) * w * sh_ref[n]
            term_o = loss_ref[p].astype(jnp.float32) * w * rest_ref[n]
            acc_i = term_i if acc_i is None else acc_i + term_i
            acc_o = term_o if acc_o is None else acc_o + term_o
        inflow = jnp.sum(acc_i, axis=0, keepdims=True)
        outflow = jnp.sum(acc_o, axis=0, keepdims=True)
        out_ref[pl.ds(m, 1), :] = (1.0 - occ[m:m + 1]) * inflow - occ[m:m + 1] * outflow


def collide(idx, near, far, weight_t, gain_t, loss_t, occ, sub_width, lanes=1024):
    pairs, shifts, width = gain_t.shape
    bands = occ.shape[0]
    sub_count = width // sub_width
    nsub = lanes // sub_width
    kern = functools.partial(collide_kernel, shifts=shifts, nsub=nsub, sub_count=sub_count,
                             sub_width=sub_width, bands=bands)
    return pl.pallas_call(
        kern,
        out_shape=jax.ShapeDtypeStruct((bands, width), jnp.float32),
        grid_spec=pltpu.PrefetchScalarGridSpec(
            num_scalar_prefetch=1,
            grid=(width // lanes,),
            in_specs=[
                pl.BlockSpec(near.shape, lambda t, i: (0, 0)),
                pl.BlockSpec(far.shape, lambda t, i: (0, 0)),
                pl.BlockSpec(weight_t.shape, lambda t, i: (0, 0, 0)),
                pl.BlockSpec((pairs, shifts, lanes), lambda t, i: (0, 0, t)),
                pl.BlockSpec((pairs, shifts, lanes), lambda t, i: (0, 0, t)),
                pl.BlockSpec((bands, lanes), lambda t, i: (0, t)),
            ],
            out_specs=pl.BlockSpec((bands, lanes), lambda t, i: (0, t)),
            scratch_shapes=[
                pltpu.VMEM((bands, shifts, lanes), jnp.float32),
                pltpu.VMEM((bands, shifts, lanes), jnp.float32),
            ],
        ),
    )(idx, near, far, weight_t, gain_t, loss_t, occ)


def ring_gather(block, y_count, z_count):
    ka_count = 2 * y_count * z_count
    per_z = 2 * y_count

    def pairs(fn):
        return [(j, fn(j)) for j in range(ka_count)]

    def y_step(d):
        return pairs(lambda j: (j // per_z) * per_z + ((j // 2 + d) % y_count) * 2 + j % 2)

    def z_step(d):
        return pairs(lambda j: ((j // per_z + d) % z_count) * per_z + j % per_z)

    def ring(x, step, count):
        ahead = {0: x}
        fwd, back = x, x
        for d in range(1, count // 2 + 1):
            back = lax.ppermute(back, "ka", step(-1))
            ahead[d] = back
            if d < count - d:
                fwd = lax.ppermute(fwd, "ka", step(1))
                ahead[count - d] = fwd
        return jnp.stack([ahead[d] for d in range(count)])

    def direct(x, step, count):
        return jnp.stack([x] + [lax.ppermute(x, "ka", step(-d)) for d in range(1, count)])

    along_y = direct(block, y_step, y_count)
    along_z = ring(along_y, z_step, z_count)
    other = lax.ppermute(along_z, "ka", pairs(lambda j: j ^ 1))
    return along_z, other


def body(occupation, gain_table, loss_table, owner, local_index, pair_mask, counts):
    bands, width = occupation.shape
    shifts = gain_table.shape[0]
    sub_count = local_index.shape[3]
    sub_width = width // sub_count
    ka_count = lax.axis_size("ka")
    pb_count = lax.axis_size("pb")
    z_count = 8
    y_count = ka_count // (2 * z_count)
    total_requests = shifts * sub_count

    local_rows = (
        occupation.reshape(bands, sub_count, sub_width)
        .transpose(1, 0, 2)
        .reshape(sub_count, bands * sub_width)
    )
    near, far = ring_gather(local_rows, y_count, z_count)
    near = near.reshape(ka_count * sub_count // 2, bands * sub_width)
    far = far.reshape(ka_count * sub_count // 2, bands * sub_width)
    me = lax.axis_index("ka")
    my_z, my_y, my_c = me // (2 * y_count), (me // 2) % y_count, me % 2
    owners = owner.reshape(total_requests)
    o_z, o_y, o_c = owners // (2 * y_count), (owners // 2) % y_count, owners % 2
    where = (
        (o_c ^ my_c) * (z_count * y_count)
        + ((o_z - my_z) % z_count) * y_count
        + (o_y - my_y) % y_count
    )
    sources = local_index.reshape(total_requests)
    picks = where * sub_count + sources
    active = (jnp.arange(shifts, dtype=jnp.int32) < counts.reshape(())).astype(jnp.float32)
    weight = pair_mask.astype(jnp.float32) * active[:, None]
    partial_terms = collide(
        picks,
        near,
        far,
        jnp.broadcast_to(weight.T[:, :, None], (bands * bands, shifts, sub_width)),
        gain_table.transpose(1, 0, 2),
        loss_table.transpose(1, 0, 2),
        occupation,
        sub_width,
    )
    share_width = width // pb_count
    parts = partial_terms.reshape(bands, pb_count, share_width).transpose(1, 0, 2)
    collision = jnp.sum(lax.all_to_all(parts, "pb", 0, 0, tiled=True), axis=0)
    own_share = lax.dynamic_slice_in_dim(
        occupation, lax.axis_index("pb") * share_width, share_width, 1
    )
    return (collision, own_share + half_step * collision)


def solution(mesh):
    return jax.shard_map(
        body,
        mesh=mesh,
        in_specs=(
            P(None, "ka"),
            P("pb", None, "ka"),
            P("pb", None, "ka"),
            P("pb", "ka", None, None, None),
            P("pb", "ka", None, None),
            P("pb", None),
            P("pb", "ka"),
        ),
        out_specs=(P(None, ("ka", "pb")), P(None, ("ka", "pb"))),
        check_vma=False,
    )
```

```python
import functools

import jax
import jax.numpy as jnp
from jax import lax
from jax.experimental import pallas as pl
from jax.experimental.pallas import tpu as pltpu
from jax.sharding import PartitionSpec as P

half_step = 0.5


def collide_kernel(idx_ref, near_ref, far_ref, last_ref, w_ref, gain_ref, loss_ref, occ_ref, out_ref, sh_ref, rest_ref,
                   *, shifts, nsub, sub_count, sub_width, bands):
    t = pl.program_id(0)
    half = near_ref.shape[0]
    early = far_ref.shape[0]
    late = last_ref.shape[0]
    for s in range(shifts):
        for jj in range(nsub):
            at = idx_ref[s * sub_count + t * nsub + jj]
            near = near_ref[pl.ds(jnp.minimum(at, half - 1), 1), :]
            far = far_ref[pl.ds(jnp.clip(at - half, 0, early - 1), 1), :]
            last = last_ref[pl.ds(jnp.clip(at - half - early, 0, late - 1), 1), :]
            row = jnp.where(at < half, near, jnp.where(at < half + early, far, last))
            for n in range(bands):
                piece = row[:, n * sub_width:(n + 1) * sub_width]
                sh_ref[n, pl.ds(s, 1), pl.ds(jj * sub_width, sub_width)] = piece
    for n in range(bands):
        rest_ref[n] = 1.0 - sh_ref[n]
    occ = occ_ref[...]
    for m in range(bands):
        acc_i = None
        acc_o = None
        for n in range(bands):
            p = m * bands + n
            w = jnp.tile(w_ref[p], (1, gain_ref.shape[2] // w_ref.shape[2]))
            term_i = gain_ref[p].astype(jnp.float32) * w * sh_ref[n]
            term_o = loss_ref[p].astype(jnp.float32) * w * rest_ref[n]
            acc_i = term_i if acc_i is None else acc_i + term_i
            acc_o = term_o if acc_o is None else acc_o + term_o
        inflow = jnp.sum(acc_i, axis=0, keepdims=True)
        outflow = jnp.sum(acc_o, axis=0, keepdims=True)
        out_ref[pl.ds(m, 1), :] = (1.0 - occ[m:m + 1]) * inflow - occ[m:m + 1] * outflow


def collide(idx, near, far, last, weight_t, gain_t, loss_t, occ, sub_width, lanes=1024):
    pairs, shifts, width = gain_t.shape
    bands = occ.shape[0]
    sub_count = width // sub_width
    nsub = lanes // sub_width
    kern = functools.partial(collide_kernel, shifts=shifts, nsub=nsub, sub_count=sub_count,
                             sub_width=sub_width, bands=bands)
    return pl.pallas_call(
        kern,
        out_shape=jax.ShapeDtypeStruct((bands, width), jnp.float32),
        grid_spec=pltpu.PrefetchScalarGridSpec(
            num_scalar_prefetch=1,
            grid=(width // lanes,),
            in_specs=[
                pl.BlockSpec(near.shape, lambda t, i: (0, 0)),
                pl.BlockSpec(far.shape, lambda t, i: (0, 0)),
                pl.BlockSpec(last.shape, lambda t, i: (0, 0)),
                pl.BlockSpec(weight_t.shape, lambda t, i: (0, 0, 0)),
                pl.BlockSpec((pairs, shifts, lanes), lambda t, i: (0, 0, t)),
                pl.BlockSpec((pairs, shifts, lanes), lambda t, i: (0, 0, t)),
                pl.BlockSpec((bands, lanes), lambda t, i: (0, t)),
            ],
            out_specs=pl.BlockSpec((bands, lanes), lambda t, i: (0, t)),
            scratch_shapes=[
                pltpu.VMEM((bands, shifts, lanes), jnp.float32),
                pltpu.VMEM((bands, shifts, lanes), jnp.float32),
            ],
        ),
    )(idx, near, far, last, weight_t, gain_t, loss_t, occ)


def ring_gather(block, y_count, z_count):
    ka_count = 2 * y_count * z_count
    per_z = 2 * y_count

    def pairs(fn):
        return [(j, fn(j)) for j in range(ka_count)]

    def y_step(d):
        return pairs(lambda j: (j // per_z) * per_z + ((j // 2 + d) % y_count) * 2 + j % 2)

    def z_step(d):
        return pairs(lambda j: ((j // per_z + d) % z_count) * per_z + j % per_z)

    def ring(x, step, count):
        ahead = {0: x}
        fwd, back = x, x
        for d in range(1, count // 2 + 1):
            back = lax.ppermute(back, "ka", step(-1))
            ahead[d] = back
            if d < count - d:
                fwd = lax.ppermute(fwd, "ka", step(1))
                ahead[count - d] = fwd
        return jnp.stack([ahead[d] for d in range(count)])

    along_y = ring(block, y_step, y_count)
    swap = pairs(lambda j: j ^ 1)
    ahead = {0: along_y}
    fwd, back = along_y, along_y
    for d in range(1, z_count // 2):
        back = lax.ppermute(back, "ka", z_step(-1))
        fwd = lax.ppermute(fwd, "ka", z_step(1))
        ahead[d] = back
        ahead[z_count - d] = fwd
    order = [d for d in range(z_count) if d != z_count // 2]
    early = jnp.stack([ahead[d] for d in order])
    early_other = lax.ppermute(early, "ka", swap)
    last = lax.ppermute(back, "ka", z_step(-1))
    last_other = lax.ppermute(last, "ka", swap)
    return jnp.concatenate([early, last[None]]), early_other, last_other


def body(occupation, gain_table, loss_table, owner, local_index, pair_mask, counts):
    bands, width = occupation.shape
    shifts = gain_table.shape[0]
    sub_count = local_index.shape[3]
    sub_width = width // sub_count
    ka_count = lax.axis_size("ka")
    pb_count = lax.axis_size("pb")
    z_count = 8
    y_count = ka_count // (2 * z_count)
    total_requests = shifts * sub_count

    local_rows = (
        occupation.reshape(bands, sub_count, sub_width)
        .transpose(1, 0, 2)
        .reshape(sub_count, bands * sub_width)
    )
    near, far, last = ring_gather(local_rows, y_count, z_count)
    near = near.reshape(-1, bands * sub_width)
    far = far.reshape(-1, bands * sub_width)
    last = last.reshape(-1, bands * sub_width)
    me = lax.axis_index("ka")
    my_z, my_y, my_c = me // (2 * y_count), (me // 2) % y_count, me % 2
    owners = owner.reshape(total_requests)
    o_z, o_y, o_c = owners // (2 * y_count), (owners // 2) % y_count, owners % 2
    dz = (o_z - my_z) % z_count
    far_z = z_count // 2
    z_slot = jnp.where(dz < far_z, dz, jnp.where(dz > far_z, dz - 1, z_count - 1))
    where = (
        (o_c ^ my_c) * (z_count * y_count)
        + z_slot * y_count
        + (o_y - my_y) % y_count
    )
    sources = local_index.reshape(total_requests)
    picks = where * sub_count + sources
    active = (jnp.arange(shifts, dtype=jnp.int32) < counts.reshape(())).astype(jnp.float32)
    weight = pair_mask.astype(jnp.float32) * active[:, None]
    partial_terms = collide(
        picks,
        near,
        far,
        last,
        jnp.broadcast_to(weight.T[:, :, None], (bands * bands, shifts, sub_width)),
        gain_table.transpose(1, 0, 2),
        loss_table.transpose(1, 0, 2),
        occupation,
        sub_width,
    )
    share_width = width // pb_count
    parts = partial_terms.reshape(bands, pb_count, share_width).transpose(1, 0, 2)
    collision = jnp.sum(lax.all_to_all(parts, "pb", 0, 0, tiled=True), axis=0)
    own_share = lax.dynamic_slice_in_dim(
        occupation, lax.axis_index("pb") * share_width, share_width, 1
    )
    return (collision, own_share + half_step * collision)


def solution(mesh):
    return jax.shard_map(
        body,
        mesh=mesh,
        in_specs=(
            P(None, "ka"),
            P("pb", None, "ka"),
            P("pb", None, "ka"),
            P("pb", "ka", None, None, None),
            P("pb", "ka", None, None),
            P("pb", None),
            P("pb", "ka"),
        ),
        out_specs=(P(None, ("ka", "pb")), P(None, ("ka", "pb"))),
        check_vma=False,
    )
```

```python
import functools

import jax
import jax.numpy as jnp
from jax import lax
from jax.experimental import pallas as pl
from jax.experimental.pallas import tpu as pltpu
from jax.sharding import PartitionSpec as P

half_step = 0.5


def collide_kernel(idx_ref, tiles_ref, near_ref, far_ref, w_ref, gain_ref, loss_ref, occ_ref, out_ref, sh_ref, rest_ref,
                   *, shifts, nsub, sub_count, sub_width, bands):
    tile = tiles_ref[pl.program_id(0)]
    half = near_ref.shape[0]
    for s in range(shifts):
        for jj in range(nsub):
            at = idx_ref[s * sub_count + tile * nsub + jj]
            near = near_ref[pl.ds(jnp.minimum(at, half - 1), 1), :]
            far = far_ref[pl.ds(jnp.maximum(at - half, 0), 1), :]
            row = jnp.where(at < half, near, far)
            for n in range(bands):
                piece = row[:, n * sub_width:(n + 1) * sub_width]
                sh_ref[n, pl.ds(s, 1), pl.ds(jj * sub_width, sub_width)] = piece
    for n in range(bands):
        rest_ref[n] = 1.0 - sh_ref[n]
    occ = occ_ref[...]
    for m in range(bands):
        acc_i = None
        acc_o = None
        for n in range(bands):
            p = m * bands + n
            w = jnp.tile(w_ref[p], (1, gain_ref.shape[2] // w_ref.shape[2]))
            term_i = gain_ref[p].astype(jnp.float32) * w * sh_ref[n]
            term_o = loss_ref[p].astype(jnp.float32) * w * rest_ref[n]
            acc_i = term_i if acc_i is None else acc_i + term_i
            acc_o = term_o if acc_o is None else acc_o + term_o
        inflow = jnp.sum(acc_i, axis=0, keepdims=True)
        outflow = jnp.sum(acc_o, axis=0, keepdims=True)
        out_ref[pl.ds(m, 1), :] = (1.0 - occ[m:m + 1]) * inflow - occ[m:m + 1] * outflow


def collide(idx, tiles, near, far, weight_t, gain_t, loss_t, occ, sub_width, lanes):
    pairs, shifts, width = gain_t.shape
    count = tiles.shape[0]
    bands = occ.shape[0]
    sub_count = width // sub_width
    nsub = lanes // sub_width
    kern = functools.partial(collide_kernel, shifts=shifts, nsub=nsub, sub_count=sub_count,
                             sub_width=sub_width, bands=bands)
    return pl.pallas_call(
        kern,
        out_shape=jax.ShapeDtypeStruct((bands, count * lanes), jnp.float32),
        grid_spec=pltpu.PrefetchScalarGridSpec(
            num_scalar_prefetch=2,
            grid=(count,),
            in_specs=[
                pl.BlockSpec(near.shape, lambda t, i, c: (0, 0)),
                pl.BlockSpec(far.shape, lambda t, i, c: (0, 0)),
                pl.BlockSpec(weight_t.shape, lambda t, i, c: (0, 0, 0)),
                pl.BlockSpec((pairs, shifts, lanes), lambda t, i, c: (0, 0, c[t])),
                pl.BlockSpec((pairs, shifts, lanes), lambda t, i, c: (0, 0, c[t])),
                pl.BlockSpec((bands, lanes), lambda t, i, c: (0, c[t])),
            ],
            out_specs=pl.BlockSpec((bands, lanes), lambda t, i, c: (0, t)),
            scratch_shapes=[
                pltpu.VMEM((bands, shifts, lanes), jnp.float32),
                pltpu.VMEM((bands, shifts, lanes), jnp.float32),
            ],
        ),
    )(idx, tiles, near, far, weight_t, gain_t, loss_t, occ)


def ring_gather(block, y_count, z_count):
    ka_count = 2 * y_count * z_count
    per_z = 2 * y_count

    def pairs(fn):
        return [(j, fn(j)) for j in range(ka_count)]

    def y_step(d):
        return pairs(lambda j: (j // per_z) * per_z + ((j // 2 + d) % y_count) * 2 + j % 2)

    def z_step(d):
        return pairs(lambda j: ((j // per_z + d) % z_count) * per_z + j % per_z)

    def ring(x, step, count):
        ahead = {0: x}
        fwd, back = x, x
        for d in range(1, count // 2 + 1):
            back = lax.ppermute(back, "ka", step(-1))
            ahead[d] = back
            if d < count - d:
                fwd = lax.ppermute(fwd, "ka", step(1))
                ahead[count - d] = fwd
        return jnp.stack([ahead[d] for d in range(count)])

    along_y = ring(block, y_step, y_count)
    along_z = ring(along_y, z_step, z_count)
    other = lax.ppermute(along_z, "ka", pairs(lambda j: j ^ 1))
    return along_z, other


def body(occupation, gain_table, loss_table, owner, local_index, pair_mask, counts):
    bands, width = occupation.shape
    shifts = gain_table.shape[0]
    sub_count = local_index.shape[3]
    sub_width = width // sub_count
    ka_count = lax.axis_size("ka")
    pb_count = lax.axis_size("pb")
    z_count = 8
    y_count = ka_count // (2 * z_count)
    total_requests = shifts * sub_count

    local_rows = (
        occupation.reshape(bands, sub_count, sub_width)
        .transpose(1, 0, 2)
        .reshape(sub_count, bands * sub_width)
    )
    near, far = ring_gather(local_rows, y_count, z_count)
    near = near.reshape(ka_count * sub_count // 2, bands * sub_width)
    far = far.reshape(ka_count * sub_count // 2, bands * sub_width)
    me = lax.axis_index("ka")
    my_z, my_y, my_c = me // (2 * y_count), (me // 2) % y_count, me % 2
    owners = owner.reshape(total_requests)
    o_z, o_y, o_c = owners // (2 * y_count), (owners // 2) % y_count, owners % 2
    where = (
        (o_c ^ my_c) * (z_count * y_count)
        + ((o_z - my_z) % z_count) * y_count
        + (o_y - my_y) % y_count
    )
    sources = local_index.reshape(total_requests)
    picks = where * sub_count + sources
    active = (jnp.arange(shifts, dtype=jnp.int32) < counts.reshape(())).astype(jnp.float32)
    weight = pair_mask.astype(jnp.float32) * active[:, None]
    lanes = 1024
    share_width = width // pb_count
    per_share = share_width // lanes
    me_pb = lax.axis_index("pb")
    step = jnp.arange(per_share, dtype=jnp.int32)
    remote = jnp.concatenate(
        [((me_pb + d) % pb_count) * per_share + step for d in range(1, pb_count)]
    )
    own = me_pb * per_share + step
    operands = (near, far, jnp.broadcast_to(weight.T[:, :, None], (bands * bands, shifts, sub_width)),
                gain_table.transpose(1, 0, 2), loss_table.transpose(1, 0, 2), occupation)
    sent = collide(picks, remote, *operands, sub_width, lanes)
    slots = jnp.concatenate([jnp.zeros((bands, share_width), jnp.float32), sent], axis=1)
    slots = slots.reshape(bands, pb_count, share_width).transpose(1, 0, 2)
    by_target = lax.dynamic_slice_in_dim(
        jnp.concatenate([slots, slots]), (pb_count - me_pb) % pb_count, pb_count, 0
    )
    received = lax.all_to_all(by_target, "pb", 0, 0, tiled=True)
    kept = collide(picks, own, *operands, sub_width, lanes)
    collision = kept + jnp.sum(received, axis=0)
    own_share = lax.dynamic_slice_in_dim(
        occupation, lax.axis_index("pb") * share_width, share_width, 1
    )
    return (collision, own_share + half_step * collision)


def solution(mesh):
    return jax.shard_map(
        body,
        mesh=mesh,
        in_specs=(
            P(None, "ka"),
            P("pb", None, "ka"),
            P("pb", None, "ka"),
            P("pb", "ka", None, None, None),
            P("pb", "ka", None, None),
            P("pb", None),
            P("pb", "ka"),
        ),
        out_specs=(P(None, ("ka", "pb")), P(None, ("ka", "pb"))),
        check_vma=False,
    )
```

```python
import functools

import jax
import jax.numpy as jnp
from jax import lax
from jax.experimental import pallas as pl
from jax.experimental.pallas import tpu as pltpu
from jax.sharding import PartitionSpec as P

half_step = 0.5


def collide_kernel(idx_ref, near_ref, far_ref, w_ref, gain_ref, loss_ref, occ_ref, out_ref, sh_ref, rest_ref,
                   *, shifts, nsub, sub_count, sub_width, bands):
    t = pl.program_id(0)
    half = near_ref.shape[0]
    for s in range(shifts):
        for jj in range(nsub):
            at = idx_ref[s * sub_count + t * nsub + jj]
            near = near_ref[pl.ds(jnp.minimum(at, half - 1), 1), :]
            far = far_ref[pl.ds(jnp.maximum(at - half, 0), 1), :]
            row = jnp.where(at < half, near, far)
            for n in range(bands):
                piece = row[:, n * sub_width:(n + 1) * sub_width]
                sh_ref[n, pl.ds(s, 1), pl.ds(jj * sub_width, sub_width)] = piece
    for n in range(bands):
        rest_ref[n] = 1.0 - sh_ref[n]
    occ = occ_ref[...]
    for m in range(bands):
        acc_i = None
        acc_o = None
        for n in range(bands):
            p = m * bands + n
            w = jnp.tile(w_ref[p], (1, gain_ref.shape[2] // w_ref.shape[2]))
            term_i = gain_ref[p].astype(jnp.float32) * w * sh_ref[n]
            term_o = loss_ref[p].astype(jnp.float32) * w * rest_ref[n]
            acc_i = term_i if acc_i is None else acc_i + term_i
            acc_o = term_o if acc_o is None else acc_o + term_o
        inflow = jnp.sum(acc_i, axis=0, keepdims=True)
        outflow = jnp.sum(acc_o, axis=0, keepdims=True)
        out_ref[pl.ds(m, 1), :] = (1.0 - occ[m:m + 1]) * inflow - occ[m:m + 1] * outflow


def collide(idx, near, far, weight_t, gain_t, loss_t, occ, sub_width, lanes=1024):
    pairs, shifts, width = gain_t.shape
    bands = occ.shape[0]
    sub_count = width // sub_width
    nsub = lanes // sub_width
    kern = functools.partial(collide_kernel, shifts=shifts, nsub=nsub, sub_count=sub_count,
                             sub_width=sub_width, bands=bands)
    return pl.pallas_call(
        kern,
        out_shape=jax.ShapeDtypeStruct((bands, width), jnp.float32),
        grid_spec=pltpu.PrefetchScalarGridSpec(
            num_scalar_prefetch=1,
            grid=(width // lanes,),
            in_specs=[
                pl.BlockSpec(near.shape, lambda t, i: (0, 0)),
                pl.BlockSpec(far.shape, lambda t, i: (0, 0)),
                pl.BlockSpec(weight_t.shape, lambda t, i: (0, 0, 0)),
                pl.BlockSpec((pairs, shifts, lanes), lambda t, i: (0, 0, t)),
                pl.BlockSpec((pairs, shifts, lanes), lambda t, i: (0, 0, t)),
                pl.BlockSpec((bands, lanes), lambda t, i: (0, t)),
            ],
            out_specs=pl.BlockSpec((bands, lanes), lambda t, i: (0, t)),
            scratch_shapes=[
                pltpu.VMEM((bands, shifts, lanes), jnp.float32),
                pltpu.VMEM((bands, shifts, lanes), jnp.float32),
            ],
        ),
    )(idx, near, far, weight_t, gain_t, loss_t, occ)


def ring_gather(block, y_count, z_count):
    ka_count = 2 * y_count * z_count
    per_z = 2 * y_count

    def pairs(fn):
        return [(j, fn(j)) for j in range(ka_count)]

    def y_step(d):
        return pairs(lambda j: (j // per_z) * per_z + ((j // 2 + d) % y_count) * 2 + j % 2)

    def z_step(d):
        return pairs(lambda j: ((j // per_z + d) % z_count) * per_z + j % per_z)

    def ring(x, step, count):
        ahead = {0: x}
        fwd, back = x, x
        for d in range(1, count // 2 + 1):
            back = lax.ppermute(back, "ka", step(-1))
            ahead[d] = back
            if d < count - d:
                fwd = lax.ppermute(fwd, "ka", step(1))
                ahead[count - d] = fwd
        return jnp.stack([ahead[d] for d in range(count)])

    along_y = ring(block, y_step, y_count)
    along_z = ring(along_y, z_step, z_count)
    other = lax.ppermute(along_z, "ka", pairs(lambda j: j ^ 1))
    return along_z, other


def body(occupation, gain_table, loss_table, owner, local_index, pair_mask, counts):
    bands, width = occupation.shape
    shifts = gain_table.shape[0]
    sub_count = local_index.shape[3]
    sub_width = width // sub_count
    ka_count = lax.axis_size("ka")
    pb_count = lax.axis_size("pb")
    z_count = 8
    y_count = ka_count // (2 * z_count)
    total_requests = shifts * sub_count

    local_rows = (
        occupation.reshape(bands, sub_count, sub_width)
        .transpose(1, 0, 2)
        .reshape(sub_count, bands * sub_width)
    )
    near, far = ring_gather(local_rows, y_count, z_count)
    near = near.reshape(ka_count * sub_count // 2, bands * sub_width)
    far = far.reshape(ka_count * sub_count // 2, bands * sub_width)
    me = lax.axis_index("ka")
    my_z, my_y, my_c = me // (2 * y_count), (me // 2) % y_count, me % 2
    owners = owner.reshape(total_requests)
    o_z, o_y, o_c = owners // (2 * y_count), (owners // 2) % y_count, owners % 2
    where = (
        (o_c ^ my_c) * (z_count * y_count)
        + ((o_z - my_z) % z_count) * y_count
        + (o_y - my_y) % y_count
    )
    sources = local_index.reshape(total_requests)
    picks = where * sub_count + sources
    active = (jnp.arange(shifts, dtype=jnp.int32) < counts.reshape(())).astype(jnp.float32)
    weight = pair_mask.astype(jnp.float32) * active[:, None]
    partial_terms = collide(
        picks,
        near,
        far,
        jnp.broadcast_to(weight.T[:, :, None], (bands * bands, shifts, sub_width)),
        gain_table.transpose(1, 0, 2),
        loss_table.transpose(1, 0, 2),
        occupation,
        sub_width,
    )
    share_width = width // pb_count
    me_pb = lax.axis_index("pb")
    collision = lax.dynamic_slice_in_dim(partial_terms, me_pb * share_width, share_width, 1)
    for d in range(1, pb_count):
        share = lax.dynamic_slice_in_dim(
            partial_terms, ((me_pb + d) % pb_count) * share_width, share_width, 1
        )
        collision = collision + lax.ppermute(
            share, "pb", [(j, (j + d) % pb_count) for j in range(pb_count)]
        )
    own_share = lax.dynamic_slice_in_dim(
        occupation, lax.axis_index("pb") * share_width, share_width, 1
    )
    return (collision, own_share + half_step * collision)


def solution(mesh):
    return jax.shard_map(
        body,
        mesh=mesh,
        in_specs=(
            P(None, "ka"),
            P("pb", None, "ka"),
            P("pb", None, "ka"),
            P("pb", "ka", None, None, None),
            P("pb", "ka", None, None),
            P("pb", None),
            P("pb", "ka"),
        ),
        out_specs=(P(None, ("ka", "pb")), P(None, ("ka", "pb"))),
        check_vma=False,
    )
```

```python
import functools

import jax
import jax.numpy as jnp
from jax import lax
from jax.experimental import pallas as pl
from jax.experimental.pallas import tpu as pltpu
from jax.sharding import PartitionSpec as P

half_step = 0.5


def collide_kernel(idx_ref, near_ref, far_ref, w_ref, gain_ref, loss_ref, occ_ref, out_ref, sh_ref, rest_ref,
                   *, shifts, nsub, sub_count, sub_width, bands):
    t = pl.program_id(0)
    half = near_ref.shape[0]
    for s in range(shifts):
        for jj in range(nsub):
            at = idx_ref[s * sub_count + t * nsub + jj]
            near = near_ref[pl.ds(jnp.minimum(at, half - 1), 1), :]
            far = far_ref[pl.ds(jnp.maximum(at - half, 0), 1), :]
            row = jnp.where(at < half, near, far)
            for n in range(bands):
                piece = row[:, n * sub_width:(n + 1) * sub_width]
                sh_ref[n, pl.ds(s, 1), pl.ds(jj * sub_width, sub_width)] = piece
    for n in range(bands):
        rest_ref[n] = 1.0 - sh_ref[n]
    occ = occ_ref[...]
    for m in range(bands):
        acc_i = None
        acc_o = None
        for n in range(bands):
            p = m * bands + n
            w = jnp.tile(w_ref[p], (1, gain_ref.shape[2] // w_ref.shape[2]))
            term_i = gain_ref[p].astype(jnp.float32) * w * sh_ref[n]
            term_o = loss_ref[p].astype(jnp.float32) * w * rest_ref[n]
            acc_i = term_i if acc_i is None else acc_i + term_i
            acc_o = term_o if acc_o is None else acc_o + term_o
        inflow = jnp.sum(acc_i, axis=0, keepdims=True)
        outflow = jnp.sum(acc_o, axis=0, keepdims=True)
        out_ref[pl.ds(m, 1), :] = (1.0 - occ[m:m + 1]) * inflow - occ[m:m + 1] * outflow


def collide(idx, near, far, weight_t, gain_t, loss_t, occ, sub_width, lanes=1024):
    pairs, shifts, width = gain_t.shape
    bands = occ.shape[0]
    sub_count = width // sub_width
    nsub = lanes // sub_width
    kern = functools.partial(collide_kernel, shifts=shifts, nsub=nsub, sub_count=sub_count,
                             sub_width=sub_width, bands=bands)
    return pl.pallas_call(
        kern,
        out_shape=jax.ShapeDtypeStruct((bands, width), jnp.float32),
        grid_spec=pltpu.PrefetchScalarGridSpec(
            num_scalar_prefetch=1,
            grid=(width // lanes,),
            in_specs=[
                pl.BlockSpec(near.shape, lambda t, i: (0, 0)),
                pl.BlockSpec(far.shape, lambda t, i: (0, 0)),
                pl.BlockSpec(weight_t.shape, lambda t, i: (0, 0, 0)),
                pl.BlockSpec((pairs, shifts, lanes), lambda t, i: (0, 0, t)),
                pl.BlockSpec((pairs, shifts, lanes), lambda t, i: (0, 0, t)),
                pl.BlockSpec((bands, lanes), lambda t, i: (0, t)),
            ],
            out_specs=pl.BlockSpec((bands, lanes), lambda t, i: (0, t)),
            scratch_shapes=[
                pltpu.VMEM((bands, shifts, lanes), jnp.float32),
                pltpu.VMEM((bands, shifts, lanes), jnp.float32),
            ],
        ),
    )(idx, near, far, weight_t, gain_t, loss_t, occ)


def ring_gather(block, y_count, z_count):
    ka_count = 2 * y_count * z_count
    per_z = 2 * y_count

    def pairs(fn):
        return [(j, fn(j)) for j in range(ka_count)]

    def y_step(d):
        return pairs(lambda j: (j // per_z) * per_z + ((j // 2 + d) % y_count) * 2 + j % 2)

    def z_step(d):
        return pairs(lambda j: ((j // per_z + d) % z_count) * per_z + j % per_z)

    def ring(x, step, count):
        ahead = {0: x}
        fwd, back = x, x
        for d in range(1, count // 2 + 1):
            back = lax.ppermute(back, "ka", step(-1))
            ahead[d] = back
            if d < count - d:
                fwd = lax.ppermute(fwd, "ka", step(1))
                ahead[count - d] = fwd
        return jnp.stack([ahead[d] for d in range(count)])

    along_y = ring(block, y_step, y_count)
    along_z = ring(along_y, z_step, z_count)
    other = lax.ppermute(along_z, "ka", pairs(lambda j: j ^ 1))
    return along_z, other


def body(occupation, gain_table, loss_table, owner, local_index, pair_mask, counts):
    bands, width = occupation.shape
    shifts = gain_table.shape[0]
    sub_count = local_index.shape[3]
    sub_width = width // sub_count
    ka_count = lax.axis_size("ka")
    pb_count = lax.axis_size("pb")
    z_count = 8
    y_count = ka_count // (2 * z_count)
    total_requests = shifts * sub_count

    local_rows = (
        occupation.reshape(bands, sub_count, sub_width)
        .transpose(1, 0, 2)
        .reshape(sub_count, bands * sub_width)
    )
    near, far = ring_gather(local_rows, y_count, z_count)
    near = near.reshape(ka_count * sub_count // 2, bands * sub_width)
    far = far.reshape(ka_count * sub_count // 2, bands * sub_width)
    me = lax.axis_index("ka")
    my_z, my_y, my_c = me // (2 * y_count), (me // 2) % y_count, me % 2
    owners = owner.reshape(total_requests)
    o_z, o_y, o_c = owners // (2 * y_count), (owners // 2) % y_count, owners % 2
    where = (
        (o_c ^ my_c) * (z_count * y_count)
        + ((o_z - my_z) % z_count) * y_count
        + (o_y - my_y) % y_count
    )
    sources = local_index.reshape(total_requests)
    picks = where * sub_count + sources
    active = (jnp.arange(shifts, dtype=jnp.int32) < counts.reshape(())).astype(jnp.float32)
    weight = pair_mask.astype(jnp.float32) * active[:, None]
    partial_terms = collide(
        picks,
        near,
        far,
        jnp.broadcast_to(weight.T[:, :, None], (bands * bands, shifts, sub_width)),
        gain_table.transpose(1, 0, 2),
        loss_table.transpose(1, 0, 2),
        occupation,
        sub_width,
    )
    share_width = width // pb_count
    me_pb = lax.axis_index("pb")
    collision = lax.dynamic_slice_in_dim(partial_terms, me_pb * share_width, share_width, 1)
    for d in sorted(range(1, pb_count), key=lambda d: -min(d, pb_count - d)):
        share = lax.dynamic_slice_in_dim(
            partial_terms, ((me_pb + d) % pb_count) * share_width, share_width, 1
        )
        collision = collision + lax.ppermute(
            share, "pb", [(j, (j + d) % pb_count) for j in range(pb_count)]
        )
    own_share = lax.dynamic_slice_in_dim(
        occupation, lax.axis_index("pb") * share_width, share_width, 1
    )
    return (collision, own_share + half_step * collision)


def solution(mesh):
    return jax.shard_map(
        body,
        mesh=mesh,
        in_specs=(
            P(None, "ka"),
            P("pb", None, "ka"),
            P("pb", None, "ka"),
            P("pb", "ka", None, None, None),
            P("pb", "ka", None, None),
            P("pb", None),
            P("pb", "ka"),
        ),
        out_specs=(P(None, ("ka", "pb")), P(None, ("ka", "pb"))),
        check_vma=False,
    )
```

```python
import functools

import jax
import jax.numpy as jnp
from jax import lax
from jax.experimental import pallas as pl
from jax.experimental.pallas import tpu as pltpu
from jax.sharding import PartitionSpec as P

half_step = 0.5


def collide_kernel(idx_ref, near_ref, far_ref, w_ref, gain_ref, loss_ref, occ_ref, out_ref, sh_ref, rest_ref,
                   *, shifts, nsub, sub_count, sub_width, bands):
    t = pl.program_id(0)
    half = near_ref.shape[0]
    for s in range(shifts):
        for jj in range(nsub):
            at = idx_ref[s * sub_count + t * nsub + jj]
            near = near_ref[pl.ds(jnp.minimum(at, half - 1), 1), :]
            far = far_ref[pl.ds(jnp.maximum(at - half, 0), 1), :]
            row = jnp.where(at < half, near, far)
            for n in range(bands):
                piece = row[:, n * sub_width:(n + 1) * sub_width]
                sh_ref[n, pl.ds(s, 1), pl.ds(jj * sub_width, sub_width)] = piece
    for n in range(bands):
        rest_ref[n] = 1.0 - sh_ref[n]
    occ = occ_ref[...]
    for m in range(bands):
        acc_i = None
        acc_o = None
        for n in range(bands):
            p = m * bands + n
            w = jnp.tile(w_ref[p], (1, gain_ref.shape[2] // w_ref.shape[2]))
            term_i = gain_ref[p].astype(jnp.float32) * w * sh_ref[n]
            term_o = loss_ref[p].astype(jnp.float32) * w * rest_ref[n]
            acc_i = term_i if acc_i is None else acc_i + term_i
            acc_o = term_o if acc_o is None else acc_o + term_o
        inflow = jnp.sum(acc_i, axis=0, keepdims=True)
        outflow = jnp.sum(acc_o, axis=0, keepdims=True)
        out_ref[0, pl.ds(m, 1), :] = (1.0 - occ[m:m + 1]) * inflow - occ[m:m + 1] * outflow


def collide(idx, near, far, weight_t, gain_t, loss_t, occ, sub_width, parts, lanes=1024):
    pairs, shifts, width = gain_t.shape
    bands = occ.shape[0]
    sub_count = width // sub_width
    nsub = lanes // sub_width
    per_part = width // parts // lanes
    kern = functools.partial(collide_kernel, shifts=shifts, nsub=nsub, sub_count=sub_count,
                             sub_width=sub_width, bands=bands)
    return pl.pallas_call(
        kern,
        out_shape=jax.ShapeDtypeStruct((parts, bands, width // parts), jnp.float32),
        grid_spec=pltpu.PrefetchScalarGridSpec(
            num_scalar_prefetch=1,
            grid=(width // lanes,),
            in_specs=[
                pl.BlockSpec(near.shape, lambda t, i: (0, 0)),
                pl.BlockSpec(far.shape, lambda t, i: (0, 0)),
                pl.BlockSpec(weight_t.shape, lambda t, i: (0, 0, 0)),
                pl.BlockSpec((pairs, shifts, lanes), lambda t, i: (0, 0, t)),
                pl.BlockSpec((pairs, shifts, lanes), lambda t, i: (0, 0, t)),
                pl.BlockSpec((bands, lanes), lambda t, i: (0, t)),
            ],
            out_specs=pl.BlockSpec(
                (1, bands, lanes), lambda t, i: (t // per_part, 0, t % per_part)
            ),
            scratch_shapes=[
                pltpu.VMEM((bands, shifts, lanes), jnp.float32),
                pltpu.VMEM((bands, shifts, lanes), jnp.float32),
            ],
        ),
    )(idx, near, far, weight_t, gain_t, loss_t, occ)


def ring_gather(block, y_count, z_count):
    ka_count = 2 * y_count * z_count
    per_z = 2 * y_count

    def pairs(fn):
        return [(j, fn(j)) for j in range(ka_count)]

    def y_step(d):
        return pairs(lambda j: (j // per_z) * per_z + ((j // 2 + d) % y_count) * 2 + j % 2)

    def z_step(d):
        return pairs(lambda j: ((j // per_z + d) % z_count) * per_z + j % per_z)

    def ring(x, step, count):
        ahead = {0: x}
        fwd, back = x, x
        for d in range(1, count // 2 + 1):
            back = lax.ppermute(back, "ka", step(-1))
            ahead[d] = back
            if d < count - d:
                fwd = lax.ppermute(fwd, "ka", step(1))
                ahead[count - d] = fwd
        return jnp.stack([ahead[d] for d in range(count)])

    along_y = ring(block, y_step, y_count)
    along_z = ring(along_y, z_step, z_count)
    other = lax.ppermute(along_z, "ka", pairs(lambda j: j ^ 1))
    return along_z, other


def body(occupation, gain_table, loss_table, owner, local_index, pair_mask, counts):
    bands, width = occupation.shape
    shifts = gain_table.shape[0]
    sub_count = local_index.shape[3]
    sub_width = width // sub_count
    ka_count = lax.axis_size("ka")
    pb_count = lax.axis_size("pb")
    z_count = 8
    y_count = ka_count // (2 * z_count)
    total_requests = shifts * sub_count

    local_rows = (
        occupation.reshape(bands, sub_count, sub_width)
        .transpose(1, 0, 2)
        .reshape(sub_count, bands * sub_width)
    )
    near, far = ring_gather(local_rows, y_count, z_count)
    near = near.reshape(ka_count * sub_count // 2, bands * sub_width)
    far = far.reshape(ka_count * sub_count // 2, bands * sub_width)
    me = lax.axis_index("ka")
    my_z, my_y, my_c = me // (2 * y_count), (me // 2) % y_count, me % 2
    owners = owner.reshape(total_requests)
    o_z, o_y, o_c = owners // (2 * y_count), (owners // 2) % y_count, owners % 2
    where = (
        (o_c ^ my_c) * (z_count * y_count)
        + ((o_z - my_z) % z_count) * y_count
        + (o_y - my_y) % y_count
    )
    sources = local_index.reshape(total_requests)
    picks = where * sub_count + sources
    active = (jnp.arange(shifts, dtype=jnp.int32) < counts.reshape(())).astype(jnp.float32)
    weight = pair_mask.astype(jnp.float32) * active[:, None]
    partial_terms = collide(
        picks,
        near,
        far,
        jnp.broadcast_to(weight.T[:, :, None], (bands * bands, shifts, sub_width)),
        gain_table.transpose(1, 0, 2),
        loss_table.transpose(1, 0, 2),
        occupation,
        sub_width,
        pb_count,
    )
    share_width = width // pb_count
    me_pb = lax.axis_index("pb")
    collision = partial_terms[me_pb]
    for d in range(1, pb_count):
        share = partial_terms[(me_pb + d) % pb_count]
        collision = collision + lax.ppermute(
            share, "pb", [(j, (j + d) % pb_count) for j in range(pb_count)]
        )
    own_share = lax.dynamic_slice_in_dim(
        occupation, lax.axis_index("pb") * share_width, share_width, 1
    )
    return (collision, own_share + half_step * collision)


def solution(mesh):
    return jax.shard_map(
        body,
        mesh=mesh,
        in_specs=(
            P(None, "ka"),
            P("pb", None, "ka"),
            P("pb", None, "ka"),
            P("pb", "ka", None, None, None),
            P("pb", "ka", None, None),
            P("pb", None),
            P("pb", "ka"),
        ),
        out_specs=(P(None, ("ka", "pb")), P(None, ("ka", "pb"))),
        check_vma=False,
    )
```
